512 devices in a mesh: expert: 32 (over z_lo, y, core), mp: 16 (over x, z_hi).
Axes of the slice: x: 4, y: 8, z: 8 (z_hi: 4, z_lo: 2; z = z_hi * 2 + z_lo), core: 2. Of those that a mesh axis runs over, the one named last changes fastest.
Arguments:
- tokens: bfloat16 [24576, 2048], P('expert', 'mp'), may hold values from -270 to 270
- norm_gain: float32 [2048], replicated, may hold values from 0.1 to 1.9
- router_weight: bfloat16 [2048, 32], replicated, may hold values from -0.125 to 0.125
- gate_proj: bfloat16 [32, 2048, 5120], P('expert', None, 'mp'), may hold values from -0.125 to 0.125
- up_proj: bfloat16 [32, 2048, 5120], P('expert', None, 'mp'), may hold values from -0.125 to 0.125
- down_proj: bfloat16 [32, 5120, 2048], P('expert', 'mp'), may hold values from -0.125 to 0.125
- expert_ids: int32 [24576], P('expert'), may hold values from 0 to 31, as said below
- slots: int32 [24576], P('expert'), may hold values from 0 to 31
- capacity: int32 [32], replicated, may hold values from 16 to 32, as said below
Outputs:
- expert_update: bfloat16 [24576, 2048], P('expert', 'mp')
The draws below stay inside these ranges and needn't reach their ends.
Inputs may be any that keep to these rules, and one draw needn't show every extreme that they name: `expert_ids`: within the 768 rows of one group no two rows name the same expert and slot; one expert, drawn from the seed, is named with every slot 0 to 31 in every group. The expert that every group fills has capacity 32.
All inputs are finite; a program needn't handle non-finite values.
Results may differ from the reference program's by a relative error of at most 0.015.
Values may be sent and summed in bfloat16 or wider, within the bound.
No kernel may reach another device: no remote copies, remote signals or barrier semaphores. Data moves between devices by JAX's collectives and lax.ppermute only.
A program may use at most 64 MiB of HBM per device.

```python
import jax
import jax.numpy as jnp
from jax import lax

D = 2048
FF = 5120
TOK_DEV = 768
EXPERTS = 32
CAP = 32
TOKENS = 24576
N_EXPERT = 32
N_MP = 16


def routing_plan(key):
    key_full, key_blocks, key_caps = jax.random.split(jax.random.fold_in(key, 7), 3)
    chosen_expert = jax.random.randint(key_full, (), 0, EXPERTS)
    cell_total = EXPERTS * CAP
    cell_expert = jnp.arange(cell_total, dtype=jnp.int32) // CAP

    def one_block(block_key):
        key_order, key_shuffle = jax.random.split(block_key)
        order = jax.random.permutation(key_order, cell_total)
        priority = order + jnp.where(cell_expert == chosen_expert, -cell_total, 0)
        picked = jnp.argsort(priority, stable=True)[:TOK_DEV]
        return jax.random.permutation(key_shuffle, picked)
    blocks = jax.vmap(one_block)(jax.random.split(key_blocks, TOKENS // TOK_DEV))
    flat_cells = blocks.reshape(TOKENS).astype(jnp.int32)
    limits = jax.random.randint(key_caps, (EXPERTS,), CAP // 2, CAP + 1)
    limits = limits.at[(chosen_expert + 1) % EXPERTS].set(CAP // 2).at[chosen_expert].set(CAP)
    return (flat_cells // CAP, flat_cells % CAP, limits.astype(jnp.int32))


def draw_expert_ids(key, part):
    return routing_plan(key)[0]


def draw_slots(key, part):
    return routing_plan(key)[1]


def draw_capacity(key, part):
    return routing_plan(key)[2]


def draw_tokens(key, part):
    key_base, key_rows, key_cols = jax.random.split(key, 3)
    ramp = jnp.exp(jnp.log(3.0) * jnp.arange(D, dtype=jnp.float32) / D)
    col_scale = ramp * jnp.exp(jax.random.uniform(key_cols, (D,), jnp.float32, jnp.log(0.4), jnp.log(4.0)))
    row_scale = jnp.exp(jax.random.uniform(key_rows, (TOKENS,), jnp.float32, jnp.log(0.5), jnp.log(5.0)))
    base = jax.random.truncated_normal(key_base, -4.0, 4.0, (TOKENS, D), jnp.float32)
    values = base * row_scale[:, None] * col_scale[None, :]
    return values.astype(jnp.bfloat16)


def raised(values, rng, source, target, shards_of, factor):
    owner, partner = [(jnp.arange(values.shape[axis_at]) // (values.shape[axis_at] // shards_of)).reshape([-1 if axis == axis_at else 1 for axis in range(values.ndim)]) for axis_at in (source, target)]
    chosen = jax.random.permutation(rng, shards_of)[partner]
    strong = (owner == chosen) | (owner == (partner + shards_of // 2) % shards_of)
    return jnp.where(strong, factor * values, values)


def block_scale(stream_key, shape, cuts, low, top_value):
    gain = 1.0
    for dim, parts in cuts:
        heights = jax.random.uniform(jax.random.fold_in(jax.random.fold_in(stream_key, 6), dim), (parts,), jnp.float32, low / len(cuts), top_value / len(cuts))
        gain = gain * jnp.repeat(jnp.exp(heights), shape[dim] // parts).reshape((-1,) + (1,) * (len(shape) - 1 - dim))
    return gain


def scatter_about(key, dims, spread, bound, shards=(), kind=jnp.bfloat16):
    entries = spread * jax.random.normal(key, dims, jnp.float32)
    if shards:
        entries = entries * block_scale(key, dims, shards, -0.22, 0.18)
    return jnp.clip(entries, -bound, bound).astype(kind)


def heavy_noise(rng, extent, spread, most, shards, heavy, held_as=jnp.bfloat16):
    array = spread * jax.random.normal(rng, extent, jnp.float32)
    if shards:
        array = array * block_scale(rng, extent, shards, -0.22, 0.18)
    return jnp.clip(raised(array, jax.random.fold_in(rng, 3), *heavy), -most, most).astype(held_as)


def setup_inputs(seed: int = 0) -> dict:
    splits = jax.random.split(jax.random.key(seed), 10)
    tokens = draw_tokens(jax.random.fold_in(splits[9], 71), 0)
    norm_gain = jnp.clip(1.0 + 0.18 * jax.random.normal(splits[1], (D,), jnp.float32), 0.1, 1.9)
    router_weight = scatter_about(splits[2], (D, EXPERTS), D ** -0.5, 0.125)
    gate_proj = scatter_about(splits[3], (EXPERTS, D, FF), D ** -0.5, 0.125, ((0, 32), (2, 16)))
    up_proj = scatter_about(splits[4], (EXPERTS, D, FF), D ** -0.5, 0.125, ((0, 32), (2, 16)))
    down_proj = heavy_noise(splits[5], (EXPERTS, FF, D), FF ** -0.5, 0.125, ((0, 32), (1, 16)), (1, 2, 16, 2.0))
    expert_ids = draw_expert_ids(jax.random.fold_in(splits[9], 71), 0)
    slots = draw_slots(jax.random.fold_in(splits[9], 71), 0)
    capacity = draw_capacity(jax.random.fold_in(splits[9], 71), 0)
    return {"tokens": tokens, "norm_gain": norm_gain, "router_weight": router_weight, "gate_proj": gate_proj, "up_proj": up_proj, "down_proj": down_proj, "expert_ids": expert_ids, "slots": slots, "capacity": capacity}


def one_expert(operands):
    rows_in, w_gate, w_up, w_down = operands
    pre_gate = jnp.dot(rows_in, w_gate, preferred_element_type=jnp.float32)
    pre_up = jnp.dot(rows_in, w_up, preferred_element_type=jnp.float32)
    hidden = (jax.nn.gelu(pre_gate, approximate=True) * pre_up).astype(jnp.bfloat16)
    blocks_in = hidden.reshape(hidden.shape[0], N_MP, FF // N_MP).astype(jnp.float32)
    blocks_w = w_down.reshape(N_MP, FF // N_MP, D).astype(jnp.float32)
    partial_value = jnp.einsum('rkf,kfd->rkd', blocks_in, blocks_w)
    rounded = lax.optimization_barrier(partial_value.astype(jnp.bfloat16))
    return lax.optimization_barrier(jnp.sum(rounded.astype(jnp.float32), axis=1)).astype(jnp.bfloat16)

def reference(tokens, norm_gain, router_weight, gate_proj, up_proj, down_proj, expert_ids, slots, capacity):
    features = tokens.astype(jnp.float32)
    mean_square = lax.optimization_barrier(jnp.mean(features * features, axis=1, keepdims=True))
    normed = (features * lax.rsqrt(mean_square + 1e-06) * norm_gain).astype(jnp.bfloat16)
    logits = jnp.dot(normed, router_weight, preferred_element_type=jnp.float32)
    onehot = expert_ids[:, None] == jnp.arange(EXPERTS, dtype=jnp.int32)[None, :]
    picked = lax.optimization_barrier(jnp.sum(jnp.where(onehot, logits, 0.0), axis=1))
    gate_prob = jax.nn.sigmoid(picked)
    kept_rows = slots < capacity[expert_ids]
    source_group = jnp.arange(TOKENS, dtype=jnp.int32) // TOK_DEV
    position = source_group * CAP + slots
    masked = jnp.where(kept_rows[:, None], normed, jnp.zeros_like(normed))
    buffer = jnp.zeros((EXPERTS, N_EXPERT * CAP, D), jnp.bfloat16).at[expert_ids, position].set(masked)
    expert_out = lax.map(one_expert, (buffer, gate_proj, up_proj, down_proj))
    gathered = expert_out[expert_ids, position].astype(jnp.float32)
    update = jnp.where(kept_rows[:, None], gate_prob[:, None] * gathered, 0.0)
    return update.astype(jnp.bfloat16)
```

```python
import jax
import jax.numpy as jnp
from jax import lax
from jax.sharding import PartitionSpec as P

norm_eps = 1e-06


def shards(
    tokens, norm_gain, router_weight, gate_proj, up_proj, down_proj, expert_ids, slots, capacity
):
    tok_rows, shard_width = tokens.shape
    model_width = norm_gain.shape[0]
    experts = router_weight.shape[1]
    n_mp = model_width // shard_width
    slot_count = 4 * tok_rows // (3 * experts)
    cells = experts * slot_count
    me = lax.axis_index("expert")

    onehot = expert_ids[:, None] == jnp.arange(experts, dtype=jnp.int32)[None, :]
    cap_token = jnp.sum(jnp.where(onehot, capacity[None, :], 0), axis=1)
    kept_rows = slots < cap_token
    target = expert_ids * slot_count + slots
    route = (
        (target[:, None] == jnp.arange(cells, dtype=jnp.int32)[None, :]) & kept_rows[:, None]
    ).astype(jnp.bfloat16)

    masked = lax.dot_general(
        route, tokens, (((0,), (0,)), ((), ())), preferred_element_type=jnp.float32
    ).astype(jnp.bfloat16)
    received = lax.all_to_all(
        masked.reshape(experts, slot_count, shard_width),
        "expert",
        split_axis=0,
        concat_axis=0,
        tiled=True,
    ).reshape(cells, shard_width)
    whole = lax.all_gather(received, "mp", axis=0, tiled=False)

    features = whole.astype(jnp.float32)
    mean_square = jnp.sum(features * features, axis=(0, 2)) / model_width
    scale = lax.rsqrt(mean_square + norm_eps)
    gain = norm_gain.reshape(n_mp, 1, shard_width)
    normed = (features * scale[None, :, None] * gain).astype(jnp.bfloat16)

    logits = lax.dot_general(
        normed,
        router_weight.reshape(n_mp, shard_width, experts),
        (((0, 2), (0, 1)), ((), ())),
        preferred_element_type=jnp.float32,
    )
    picked = jnp.sum(
        jnp.where(jnp.arange(experts, dtype=jnp.int32)[None, :] == me, logits, 0.0), axis=1
    )
    gate_prob = jax.nn.sigmoid(picked)

    ff_local = gate_proj.shape[2]
    w_gate = gate_proj[0].reshape(n_mp, shard_width, ff_local)
    w_up = up_proj[0].reshape(n_mp, shard_width, ff_local)
    dims = (((0, 2), (0, 1)), ((), ()))
    pre_gate = lax.dot_general(normed, w_gate, dims, preferred_element_type=jnp.float32)
    pre_up = lax.dot_general(normed, w_up, dims, preferred_element_type=jnp.float32)
    hidden = (jax.nn.gelu(pre_gate, approximate=True) * pre_up).astype(jnp.bfloat16)
    block_out = jnp.dot(hidden, down_proj[0], preferred_element_type=jnp.float32).astype(
        jnp.bfloat16
    )
    summed = lax.psum_scatter(block_out, "mp", scatter_dimension=1, tiled=True)
    gated = (gate_prob[:, None] * summed.astype(jnp.float32)).astype(jnp.bfloat16)

    returned = lax.all_to_all(
        gated.reshape(experts, slot_count, shard_width),
        "expert",
        split_axis=0,
        concat_axis=0,
        tiled=True,
    ).reshape(cells, shard_width)
    update = jnp.dot(route, returned, preferred_element_type=jnp.float32)
    return update.astype(jnp.bfloat16)


def solution(mesh):
    in_specs = (
        P("expert", "mp"),
        P(),
        P(),
        P("expert", None, "mp"),
        P("expert", None, "mp"),
        P("expert", "mp", None),
        P("expert"),
        P("expert"),
        P(),
    )
    out_specs = P("expert", "mp")
    return jax.shard_map(shards, mesh=mesh, in_specs=in_specs, out_specs=out_specs, check_vma=False)
```

```python
import jax
import jax.numpy as jnp
from jax import lax
from jax.sharding import Mesh, PartitionSpec as P

norm_eps = 1e-06


def shards(
    tokens, norm_gain, router_weight, gate_proj, up_proj, down_proj, expert_ids, slots, capacity
):
    tok_rows, shard_width = tokens.shape
    model_width = norm_gain.shape[0]
    experts = router_weight.shape[1]
    n_mp = model_width // shard_width
    slot_count = 4 * tok_rows // (3 * experts)
    cells = experts * slot_count
    me = lax.axis_index("expert")

    onehot = expert_ids[:, None] == jnp.arange(experts, dtype=jnp.int32)[None, :]
    cap_token = jnp.sum(jnp.where(onehot, capacity[None, :], 0), axis=1)
    kept_rows = slots < cap_token
    target = expert_ids * slot_count + slots
    route = (
        (target[:, None] == jnp.arange(cells, dtype=jnp.int32)[None, :]) & kept_rows[:, None]
    ).astype(jnp.bfloat16)

    masked = lax.dot_general(
        route, tokens, (((0,), (0,)), ((), ())), preferred_element_type=jnp.float32
    ).astype(jnp.bfloat16)
    received = lax.all_to_all(
        masked.reshape(experts, slot_count, shard_width),
        "expert",
        split_axis=0,
        concat_axis=0,
        tiled=True,
    ).reshape(cells, shard_width)
    part = lax.all_gather(received, "mz", axis=0, tiled=False)
    whole = lax.all_gather(part, "mx", axis=0, tiled=False).reshape(n_mp, cells, shard_width)

    features = whole.astype(jnp.float32)
    mean_square = jnp.sum(features * features, axis=(0, 2)) / model_width
    scale = lax.rsqrt(mean_square + norm_eps)
    gain = norm_gain.reshape(n_mp, 1, shard_width)
    normed = (features * scale[None, :, None] * gain).astype(jnp.bfloat16)

    logits = lax.dot_general(
        normed,
        router_weight.reshape(n_mp, shard_width, experts),
        (((0, 2), (0, 1)), ((), ())),
        preferred_element_type=jnp.float32,
    )
    picked = jnp.sum(
        jnp.where(jnp.arange(experts, dtype=jnp.int32)[None, :] == me, logits, 0.0), axis=1
    )
    gate_prob = jax.nn.sigmoid(picked)

    ff_local = gate_proj.shape[2]
    w_gate = gate_proj[0].reshape(n_mp, shard_width, ff_local)
    w_up = up_proj[0].reshape(n_mp, shard_width, ff_local)
    dims = (((0, 2), (0, 1)), ((), ()))
    pre_gate = lax.dot_general(normed, w_gate, dims, preferred_element_type=jnp.float32)
    pre_up = lax.dot_general(normed, w_up, dims, preferred_element_type=jnp.float32)
    hidden = (jax.nn.gelu(pre_gate, approximate=True) * pre_up).astype(jnp.bfloat16)
    block_out = jnp.dot(hidden, down_proj[0], preferred_element_type=jnp.float32).astype(
        jnp.bfloat16
    )
    half = lax.psum_scatter(block_out, "mx", scatter_dimension=1, tiled=True)
    summed = lax.psum_scatter(half, "mz", scatter_dimension=1, tiled=True)
    gated = (gate_prob[:, None] * summed.astype(jnp.float32)).astype(jnp.bfloat16)

    returned = lax.all_to_all(
        gated.reshape(experts, slot_count, shard_width),
        "expert",
        split_axis=0,
        concat_axis=0,
        tiled=True,
    ).reshape(cells, shard_width)
    update = jnp.dot(route, returned, preferred_element_type=jnp.float32)
    return update.astype(jnp.bfloat16)


def solution(mesh):
    n_expert, n_mp = mesh.devices.shape
    n_x = len({device.coords[0] for device in mesh.devices[0]})
    split = Mesh(mesh.devices.reshape(n_expert, n_x, n_mp // n_x), ("expert", "mx", "mz"))
    mp = ("mx", "mz")
    in_specs = (
        P("expert", mp),
        P(),
        P(),
        P("expert", None, mp),
        P("expert", None, mp),
        P("expert", mp, None),
        P("expert"),
        P("expert"),
        P(),
    )
    out_specs = P("expert", mp)
    return jax.shard_map(shards, mesh=split, in_specs=in_specs, out_specs=out_specs, check_vma=False)
```

```python
import jax
import jax.numpy as jnp
from jax import lax
from jax.sharding import Mesh, PartitionSpec as P

norm_eps = 1e-06


def shift(value, axis, n, step):
    return lax.ppermute(value, axis, [(i, (i + step) % n) for i in range(n)])


def ring_gather(block, axis, n):
    if n == 1:
        return block[None]
    me = lax.axis_index(axis)
    half = block.shape[0] // 2
    pieces = [None] * n
    pieces[0] = block
    rightward = leftward = block
    for step in range(1, (n + 1) // 2):
        rightward = shift(rightward, axis, n, 1)
        leftward = shift(leftward, axis, n, -1)
        pieces[n - step] = rightward
        pieces[step] = leftward
    if n % 2 == 0:
        first = shift(rightward[:half], axis, n, 1)
        second = shift(leftward[half:], axis, n, -1)
        pieces[n // 2] = jnp.concatenate([first, second], axis=0)
    return jnp.roll(jnp.stack(pieces), me, axis=0)


def ring_reduce_scatter(parts, axis, n):
    if n == 1:
        return parts[:, 0].astype(jnp.float32)
    me = lax.axis_index(axis)
    half = parts.shape[0] // 2

    def term(dest, lower):
        rows = parts[:half] if lower else parts[half:]
        return lax.dynamic_index_in_dim(rows, dest % n, axis=1, keepdims=False)

    results = []
    for lower, direction in ((True, 1), (False, -1)):
        carried = term(me - direction, lower)
        for step in range(1, n):
            arrived = shift(carried, axis, n, direction)
            total = arrived.astype(jnp.float32) + term(
                me - direction * (step + 1), lower
            ).astype(jnp.float32)
            carried = total.astype(parts.dtype) if step < n - 1 else total
        results.append(carried)
    return jnp.concatenate(results, axis=0)


def shards(
    tokens, norm_gain, router_weight, gate_proj, up_proj, down_proj, expert_ids, slots, capacity
):
    tok_rows, shard_width = tokens.shape
    model_width = norm_gain.shape[0]
    experts = router_weight.shape[1]
    n_mp = model_width // shard_width
    slot_count = 4 * tok_rows // (3 * experts)
    cells = experts * slot_count
    me = lax.axis_index("expert")

    onehot = expert_ids[:, None] == jnp.arange(experts, dtype=jnp.int32)[None, :]
    cap_token = jnp.sum(jnp.where(onehot, capacity[None, :], 0), axis=1)
    kept_rows = slots < cap_token
    target = expert_ids * slot_count + slots
    route = (
        (target[:, None] == jnp.arange(cells, dtype=jnp.int32)[None, :]) & kept_rows[:, None]
    ).astype(jnp.bfloat16)

    masked = lax.dot_general(
        route, tokens, (((0,), (0,)), ((), ())), preferred_element_type=jnp.float32
    ).astype(jnp.bfloat16)
    received = lax.all_to_all(
        masked.reshape(experts, slot_count, shard_width),
        "expert",
        split_axis=0,
        concat_axis=0,
        tiled=True,
    ).reshape(cells, shard_width)
    n_z = lax.psum(1, "mz")
    n_x = n_mp // n_z
    part = ring_gather(received, "mz", n_z)
    whole = ring_gather(part, "mx", n_x).reshape(n_mp, cells, shard_width)

    features = whole.astype(jnp.float32)
    mean_square = jnp.sum(features * features, axis=(0, 2)) / model_width
    scale = lax.rsqrt(mean_square + norm_eps)
    gain = norm_gain.reshape(n_mp, 1, shard_width)
    normed = (features * scale[None, :, None] * gain).astype(jnp.bfloat16)

    logits = lax.dot_general(
        normed,
        router_weight.reshape(n_mp, shard_width, experts),
        (((0, 2), (0, 1)), ((), ())),
        preferred_element_type=jnp.float32,
    )
    picked = jnp.sum(
        jnp.where(jnp.arange(experts, dtype=jnp.int32)[None, :] == me, logits, 0.0), axis=1
    )
    gate_prob = jax.nn.sigmoid(picked)

    ff_local = gate_proj.shape[2]
    w_gate = gate_proj[0].reshape(n_mp, shard_width, ff_local)
    w_up = up_proj[0].reshape(n_mp, shard_width, ff_local)
    dims = (((0, 2), (0, 1)), ((), ()))
    pre_gate = lax.dot_general(normed, w_gate, dims, preferred_element_type=jnp.float32)
    pre_up = lax.dot_general(normed, w_up, dims, preferred_element_type=jnp.float32)
    hidden = (jax.nn.gelu(pre_gate, approximate=True) * pre_up).astype(jnp.bfloat16)
    block_out = jnp.dot(hidden, down_proj[0], preferred_element_type=jnp.float32).astype(
        jnp.bfloat16
    )
    across_x = ring_reduce_scatter(block_out.reshape(cells, n_x, -1), "mx", n_x)
    summed = ring_reduce_scatter(
        across_x.astype(jnp.bfloat16).reshape(cells, n_z, shard_width), "mz", n_z
    ).astype(jnp.bfloat16)
    gated = (gate_prob[:, None] * summed.astype(jnp.float32)).astype(jnp.bfloat16)

    returned = lax.all_to_all(
        gated.reshape(experts, slot_count, shard_width),
        "expert",
        split_axis=0,
        concat_axis=0,
        tiled=True,
    ).reshape(cells, shard_width)
    update = jnp.dot(route, returned, preferred_element_type=jnp.float32)
    return update.astype(jnp.bfloat16)


def solution(mesh):
    n_expert, n_mp = mesh.devices.shape
    n_x = len({device.coords[0] for device in mesh.devices[0]})
    split = Mesh(mesh.devices.reshape(n_expert, n_x, n_mp // n_x), ("expert", "mx", "mz"))
    mp = ("mx", "mz")
    in_specs = (
        P("expert", mp),
        P(),
        P(),
        P("expert", None, mp),
        P("expert", None, mp),
        P("expert", mp, None),
        P("expert"),
        P("expert"),
        P(),
    )
    out_specs = P("expert", mp)
    return jax.shard_map(shards, mesh=split, in_specs=in_specs, out_specs=out_specs, check_vma=False)
```

```python
import jax
import jax.numpy as jnp
from jax import lax
from jax.sharding import Mesh, PartitionSpec as P

norm_eps = 1e-06


def shift(value, axis, n, step):
    return lax.ppermute(value, axis, [(i, (i + step) % n) for i in range(n)])


def ring_gather(block, axis, n):
    if n == 1:
        return block[None]
    half = block.shape[0] // 2
    pieces = [None] * n
    pieces[0] = block
    rightward = leftward = block
    for step in range(1, (n + 1) // 2):
        rightward = shift(rightward, axis, n, 1)
        leftward = shift(leftward, axis, n, -1)
        pieces[n - step] = rightward
        pieces[step] = leftward
    if n % 2 == 0:
        first = shift(rightward[:half], axis, n, 1)
        second = shift(leftward[half:], axis, n, -1)
        pieces[n // 2] = jnp.concatenate([first, second], axis=0)
    return jnp.stack(pieces)


def ring_reduce_scatter(parts, axis, n):
    if n == 1:
        return parts[:, 0].astype(jnp.float32)
    half = parts.shape[0] // 2

    def term(offset, lower):
        rows = parts[:half] if lower else parts[half:]
        return rows[:, offset % n]

    results = []
    for lower, direction in ((True, 1), (False, -1)):
        carried = term(-direction, lower)
        for step in range(1, n):
            arrived = shift(carried, axis, n, direction)
            total = arrived.astype(jnp.float32) + term(-direction * (step + 1), lower).astype(
                jnp.float32
            )
            carried = total.astype(parts.dtype) if step < n - 1 else total
        results.append(carried)
    return jnp.concatenate(results, axis=0)


def shards(
    tokens, norm_gain, router_weight, gate_proj, up_proj, down_proj, expert_ids, slots, capacity
):
    tok_rows, shard_width = tokens.shape
    model_width = norm_gain.shape[0]
    experts = router_weight.shape[1]
    n_mp = model_width // shard_width
    slot_count = 4 * tok_rows // (3 * experts)
    cells = experts * slot_count
    me = lax.axis_index("expert")

    onehot = expert_ids[:, None] == jnp.arange(experts, dtype=jnp.int32)[None, :]
    cap_token = jnp.sum(jnp.where(onehot, capacity[None, :], 0), axis=1)
    kept_rows = slots < cap_token
    target = expert_ids * slot_count + slots
    route = (
        (target[:, None] == jnp.arange(cells, dtype=jnp.int32)[None, :]) & kept_rows[:, None]
    ).astype(jnp.bfloat16)

    masked = lax.dot_general(
        route, tokens, (((0,), (0,)), ((), ())), preferred_element_type=jnp.float32
    ).astype(jnp.bfloat16)
    received = lax.all_to_all(
        masked.reshape(experts, slot_count, shard_width),
        "expert",
        split_axis=0,
        concat_axis=0,
        tiled=True,
    ).reshape(cells, shard_width)
    n_z = lax.psum(1, "mz")
    n_x = n_mp // n_z
    at_x, at_z = lax.axis_index("mx"), lax.axis_index("mz")

    def relative(blocks, axes):
        return jnp.roll(blocks, (-at_x, -at_z), axis=axes)

    part = ring_gather(received, "mz", n_z)
    whole = ring_gather(part, "mx", n_x).reshape(n_mp, cells, shard_width)

    features = whole.astype(jnp.float32)
    mean_square = jnp.sum(features * features, axis=(0, 2)) / model_width
    scale = lax.rsqrt(mean_square + norm_eps)
    gain = relative(norm_gain.reshape(n_x, n_z, shard_width), (0, 1)).reshape(n_mp, 1, shard_width)
    normed = (features * scale[None, :, None] * gain).astype(jnp.bfloat16)

    logits = lax.dot_general(
        normed,
        relative(router_weight.reshape(n_x, n_z, shard_width, experts), (0, 1)).reshape(
            n_mp, shard_width, experts
        ),
        (((0, 2), (0, 1)), ((), ())),
        preferred_element_type=jnp.float32,
    )
    picked = jnp.sum(
        jnp.where(jnp.arange(experts, dtype=jnp.int32)[None, :] == me, logits, 0.0), axis=1
    )
    gate_prob = jax.nn.sigmoid(picked)

    ff_local = gate_proj.shape[2]
    w_gate = relative(gate_proj[0].reshape(n_x, n_z, shard_width, ff_local), (0, 1))
    w_up = relative(up_proj[0].reshape(n_x, n_z, shard_width, ff_local), (0, 1))
    w_gate = w_gate.reshape(n_mp, shard_width, ff_local)
    w_up = w_up.reshape(n_mp, shard_width, ff_local)
    w_down = relative(down_proj[0].reshape(ff_local, n_x, n_z, shard_width), (1, 2))
    dims = (((0, 2), (0, 1)), ((), ()))
    pre_gate = lax.dot_general(normed, w_gate, dims, preferred_element_type=jnp.float32)
    pre_up = lax.dot_general(normed, w_up, dims, preferred_element_type=jnp.float32)
    hidden = (jax.nn.gelu(pre_gate, approximate=True) * pre_up).astype(jnp.bfloat16)
    block_out = jnp.dot(
        hidden, w_down.reshape(ff_local, model_width), preferred_element_type=jnp.float32
    ).astype(jnp.bfloat16)
    across_x = ring_reduce_scatter(block_out.reshape(cells, n_x, -1), "mx", n_x)
    summed = ring_reduce_scatter(
        across_x.astype(jnp.bfloat16).reshape(cells, n_z, shard_width), "mz", n_z
    ).astype(jnp.bfloat16)
    gated = (gate_prob[:, None] * summed.astype(jnp.float32)).astype(jnp.bfloat16)

    returned = lax.all_to_all(
        gated.reshape(experts, slot_count, shard_width),
        "expert",
        split_axis=0,
        concat_axis=0,
        tiled=True,
    ).reshape(cells, shard_width)
    update = jnp.dot(route, returned, preferred_element_type=jnp.float32)
    return update.astype(jnp.bfloat16)


def solution(mesh):
    n_expert, n_mp = mesh.devices.shape
    n_x = len({device.coords[0] for device in mesh.devices[0]})
    split = Mesh(mesh.devices.reshape(n_expert, n_x, n_mp // n_x), ("expert", "mx", "mz"))
    mp = ("mx", "mz")
    in_specs = (
        P("expert", mp),
        P(),
        P(),
        P("expert", None, mp),
        P("expert", None, mp),
        P("expert", mp, None),
        P("expert"),
        P("expert"),
        P(),
    )
    out_specs = P("expert", mp)
    return jax.shard_map(shards, mesh=split, in_specs=in_specs, out_specs=out_specs, check_vma=False)
```

```python
import jax
import jax.numpy as jnp
from jax import lax
from jax.sharding import Mesh, PartitionSpec as P

norm_eps = 1e-06


def shift(value, axis, n, step):
    return lax.ppermute(value, axis, [(i, (i + step) % n) for i in range(n)])


def ring_gather(block, axis, n):
    if n == 1:
        return block[None]
    half = block.shape[0] // 2
    pieces = [None] * n
    pieces[0] = block
    rightward = leftward = block
    for step in range(1, (n + 1) // 2):
        rightward = shift(rightward, axis, n, 1)
        leftward = shift(leftward, axis, n, -1)
        pieces[n - step] = rightward
        pieces[step] = leftward
    if n % 2 == 0:
        first = shift(rightward[:half], axis, n, 1)
        second = shift(leftward[half:], axis, n, -1)
        pieces[n // 2] = jnp.concatenate([first, second], axis=0)
    return jnp.stack(pieces)


def ring_reduce_scatter(term, axis, n):
    if n == 1:
        return [term(0, True).astype(jnp.float32), term(0, False).astype(jnp.float32)]
    results = []
    for lower, direction in ((True, 1), (False, -1)):
        carried = term(-direction % n, lower)
        for step in range(1, n):
            arrived = shift(carried, axis, n, direction)
            own = term((-direction * (step + 1)) % n, lower)
            total = arrived.astype(jnp.float32) + own.astype(jnp.float32)
            carried = total.astype(own.dtype) if step < n - 1 else total
        results.append(carried)
    return results


def shards(
    tokens, norm_gain, router_weight, gate_proj, up_proj, down_proj, expert_ids, slots, capacity
):
    tok_rows, shard_width = tokens.shape
    model_width = norm_gain.shape[0]
    experts = router_weight.shape[1]
    n_mp = model_width // shard_width
    slot_count = 4 * tok_rows // (3 * experts)
    cells = experts * slot_count
    me = lax.axis_index("expert")

    onehot = expert_ids[:, None] == jnp.arange(experts, dtype=jnp.int32)[None, :]
    cap_token = jnp.sum(jnp.where(onehot, capacity[None, :], 0), axis=1)
    kept_rows = slots < cap_token
    target = expert_ids * slot_count + slots
    route = (
        (target[:, None] == jnp.arange(cells, dtype=jnp.int32)[None, :]) & kept_rows[:, None]
    ).astype(jnp.bfloat16)

    masked = lax.dot_general(
        route, tokens, (((0,), (0,)), ((), ())), preferred_element_type=jnp.float32
    ).astype(jnp.bfloat16)
    received = lax.all_to_all(
        masked.reshape(experts, slot_count, shard_width),
        "expert",
        split_axis=0,
        concat_axis=0,
        tiled=True,
    ).reshape(cells, shard_width)
    n_z = lax.psum(1, "mz")
    n_x = n_mp // n_z
    at_x, at_z = lax.axis_index("mx"), lax.axis_index("mz")

    def relative(blocks, axes):
        return jnp.roll(blocks, (-at_x, -at_z), axis=axes)

    part = ring_gather(received, "mz", n_z)
    whole = ring_gather(part, "mx", n_x).reshape(n_mp, cells, shard_width)

    features = whole.astype(jnp.float32)
    mean_square = jnp.sum(features * features, axis=(0, 2)) / model_width
    scale = lax.rsqrt(mean_square + norm_eps)
    gain = relative(norm_gain.reshape(n_x, n_z, shard_width), (0, 1)).reshape(n_mp, 1, shard_width)
    normed = (features * scale[None, :, None] * gain).astype(jnp.bfloat16)

    logits = lax.dot_general(
        normed,
        relative(router_weight.reshape(n_x, n_z, shard_width, experts), (0, 1)).reshape(
            n_mp, shard_width, experts
        ),
        (((0, 2), (0, 1)), ((), ())),
        preferred_element_type=jnp.float32,
    )
    picked = jnp.sum(
        jnp.where(jnp.arange(experts, dtype=jnp.int32)[None, :] == me, logits, 0.0), axis=1
    )
    gate_prob = jax.nn.sigmoid(picked)

    ff_local = gate_proj.shape[2]
    w_gate = relative(gate_proj[0].reshape(n_x, n_z, shard_width, ff_local), (0, 1))
    w_up = relative(up_proj[0].reshape(n_x, n_z, shard_width, ff_local), (0, 1))
    w_gate = w_gate.reshape(n_mp, shard_width, ff_local)
    w_up = w_up.reshape(n_mp, shard_width, ff_local)
    w_down = relative(down_proj[0].reshape(ff_local, n_x, n_z, shard_width), (1, 2))
    dims = (((0, 2), (0, 1)), ((), ()))
    pre_gate = lax.dot_general(normed, w_gate, dims, preferred_element_type=jnp.float32)
    pre_up = lax.dot_general(normed, w_up, dims, preferred_element_type=jnp.float32)
    hidden = (jax.nn.gelu(pre_gate, approximate=True) * pre_up).astype(jnp.bfloat16)
    rows_half = cells // 2
    hidden_halves = {True: hidden[:rows_half], False: hidden[rows_half:]}
    w_down = w_down.reshape(ff_local, n_x, n_z * shard_width)

    def x_term(k, lower):
        return jnp.dot(
            hidden_halves[lower], w_down[:, k], preferred_element_type=jnp.float32
        ).astype(jnp.bfloat16)

    across_x = [part.astype(jnp.bfloat16) for part in ring_reduce_scatter(x_term, "mx", n_x)]

    def z_term(k, lower):
        return across_x[0 if lower else 1][:, k * shard_width : (k + 1) * shard_width]

    summed = jnp.concatenate(ring_reduce_scatter(z_term, "mz", n_z), axis=0).astype(jnp.bfloat16)
    gated = (gate_prob[:, None] * summed.astype(jnp.float32)).astype(jnp.bfloat16)

    returned = lax.all_to_all(
        gated.reshape(experts, slot_count, shard_width),
        "expert",
        split_axis=0,
        concat_axis=0,
        tiled=True,
    ).reshape(cells, shard_width)
    update = jnp.dot(route, returned, preferred_element_type=jnp.float32)
    return update.astype(jnp.bfloat16)


def solution(mesh):
    n_expert, n_mp = mesh.devices.shape
    n_x = len({device.coords[0] for device in mesh.devices[0]})
    split = Mesh(mesh.devices.reshape(n_expert, n_x, n_mp // n_x), ("expert", "mx", "mz"))
    mp = ("mx", "mz")
    in_specs = (
        P("expert", mp),
        P(),
        P(),
        P("expert", None, mp),
        P("expert", None, mp),
        P("expert", mp, None),
        P("expert"),
        P("expert"),
        P(),
    )
    out_specs = P("expert", mp)
    return jax.shard_map(shards, mesh=split, in_specs=in_specs, out_specs=out_specs, check_vma=False)
```

```python
import jax
import jax.numpy as jnp
from jax import lax
from jax.sharding import Mesh, PartitionSpec as P

norm_eps = 1e-06


def shift(value, axis, n, step):
    return lax.ppermute(value, axis, [(i, (i + step) % n) for i in range(n)])


def ring_gather(block, axis, n):
    if n == 1:
        return block[None]
    half = block.shape[0] // 2
    pieces = [None] * n
    pieces[0] = block
    rightward = leftward = block
    for step in range(1, (n + 1) // 2):
        rightward = shift(rightward, axis, n, 1)
        leftward = shift(leftward, axis, n, -1)
        pieces[n - step] = rightward
        pieces[step] = leftward
    if n % 2 == 0:
        first = shift(rightward[:half], axis, n, 1)
        second = shift(leftward[half:], axis, n, -1)
        pieces[n // 2] = jnp.concatenate([first, second], axis=0)
    return jnp.stack(pieces)


def ring_reduce_scatter(term, axis, n):
    if n == 1:
        return [term(0, True).astype(jnp.float32), term(0, False).astype(jnp.float32)]
    results = []
    for lower, direction in ((True, 1), (False, -1)):
        carried = term(-direction % n, lower)
        for step in range(1, n):
            arrived = shift(carried, axis, n, direction)
            own = term((-direction * (step + 1)) % n, lower)
            total = arrived.astype(jnp.float32) + own.astype(jnp.float32)
            carried = total.astype(own.dtype) if step < n - 1 else total
        results.append(carried)
    return results


def shards(
    tokens, norm_gain, router_weight, gate_proj, up_proj, down_proj, expert_ids, slots, capacity
):
    tok_rows, shard_width = tokens.shape
    model_width = norm_gain.shape[0]
    experts = router_weight.shape[1]
    n_mp = model_width // shard_width
    slot_count = 4 * tok_rows // (3 * experts)
    cells = experts * slot_count
    me = lax.axis_index("expert")

    onehot = expert_ids[:, None] == jnp.arange(experts, dtype=jnp.int32)[None, :]
    cap_token = jnp.sum(jnp.where(onehot, capacity[None, :], 0), axis=1)
    kept_rows = slots < cap_token
    target = expert_ids * slot_count + slots
    route = (
        (target[:, None] == jnp.arange(cells, dtype=jnp.int32)[None, :]) & kept_rows[:, None]
    ).astype(jnp.bfloat16)

    masked = lax.dot_general(
        route, tokens, (((0,), (0,)), ((), ())), preferred_element_type=jnp.float32
    ).astype(jnp.bfloat16)
    received = lax.all_to_all(
        masked.reshape(experts, slot_count, shard_width),
        "expert",
        split_axis=0,
        concat_axis=0,
        tiled=True,
    ).reshape(cells, shard_width)
    n_z = lax.psum(1, "mz")
    n_x = n_mp // n_z
    at_x, at_z = lax.axis_index("mx"), lax.axis_index("mz")

    def rows_relative(w):
        lead = w.shape[0]
        w = jnp.roll(w, -at_x * (lead // n_x), axis=0)
        w = jnp.roll(w.reshape(n_x, lead // n_x, *w.shape[1:]), -at_z * (lead // n_mp), axis=1)
        return w.reshape(lead, *w.shape[2:])

    part = ring_gather(received, "mz", n_z)
    whole = ring_gather(part, "mx", n_x).reshape(n_mp, cells, shard_width)

    features = jnp.transpose(whole, (1, 0, 2)).reshape(cells, model_width).astype(jnp.float32)
    mean_square = jnp.sum(features * features, axis=1) / model_width
    scale = lax.rsqrt(mean_square + norm_eps)
    normed = (features * scale[:, None] * rows_relative(norm_gain)).astype(jnp.bfloat16)

    logits = jnp.dot(normed, rows_relative(router_weight), preferred_element_type=jnp.float32)
    picked = jnp.sum(
        jnp.where(jnp.arange(experts, dtype=jnp.int32)[None, :] == me, logits, 0.0), axis=1
    )
    gate_prob = jax.nn.sigmoid(picked)

    ff_local = gate_proj.shape[2]
    pre_gate = jnp.dot(normed, rows_relative(gate_proj[0]), preferred_element_type=jnp.float32)
    pre_up = jnp.dot(normed, rows_relative(up_proj[0]), preferred_element_type=jnp.float32)
    hidden = (jax.nn.gelu(pre_gate, approximate=True) * pre_up).astype(jnp.bfloat16)
    rows_half = cells // 2
    hidden_halves = {True: hidden[:rows_half], False: hidden[rows_half:]}
    x_width = model_width // n_x

    def x_term(k, lower):
        columns = lax.dynamic_slice_in_dim(
            down_proj[0], ((at_x + k) % n_x) * x_width, x_width, axis=1
        )
        return jnp.dot(hidden_halves[lower], columns, preferred_element_type=jnp.float32).astype(
            jnp.bfloat16
        )

    across_x = [part.astype(jnp.bfloat16) for part in ring_reduce_scatter(x_term, "mx", n_x)]

    def z_term(k, lower):
        return lax.dynamic_slice_in_dim(
            across_x[0 if lower else 1], ((at_z + k) % n_z) * shard_width, shard_width, axis=1
        )

    summed = jnp.concatenate(ring_reduce_scatter(z_term, "mz", n_z), axis=0).astype(jnp.bfloat16)
    gated = (gate_prob[:, None] * summed.astype(jnp.float32)).astype(jnp.bfloat16)

    returned = lax.all_to_all(
        gated.reshape(experts, slot_count, shard_width),
        "expert",
        split_axis=0,
        concat_axis=0,
        tiled=True,
    ).reshape(cells, shard_width)
    update = jnp.dot(route, returned, preferred_element_type=jnp.float32)
    return update.astype(jnp.bfloat16)


def solution(mesh):
    n_expert, n_mp = mesh.devices.shape
    n_x = len({device.coords[0] for device in mesh.devices[0]})
    split = Mesh(mesh.devices.reshape(n_expert, n_x, n_mp // n_x), ("expert", "mx", "mz"))
    mp = ("mx", "mz")
    in_specs = (
        P("expert", mp),
        P(),
        P(),
        P("expert", None, mp),
        P("expert", None, mp),
        P("expert", mp, None),
        P("expert"),
        P("expert"),
        P(),
    )
    out_specs = P("expert", mp)
    return jax.shard_map(shards, mesh=split, in_specs=in_specs, out_specs=out_specs, check_vma=False)
```

```python
import jax
import jax.numpy as jnp
from jax import lax
from jax.sharding import Mesh, PartitionSpec as P

norm_eps = 1e-06


def shift(value, axis, n, step):
    return lax.ppermute(value, axis, [(i, (i + step) % n) for i in range(n)])


def ring_gather(block, axis, n):
    if n == 1:
        return block[None]
    half = block.shape[0] // 2
    pieces = [None] * n
    pieces[0] = block
    rightward = leftward = block
    for step in range(1, (n + 1) // 2):
        rightward = shift(rightward, axis, n, 1)
        leftward = shift(leftward, axis, n, -1)
        pieces[n - step] = rightward
        pieces[step] = leftward
    if n % 2 == 0:
        first = shift(rightward[:half], axis, n, 1)
        second = shift(leftward[half:], axis, n, -1)
        pieces[n // 2] = jnp.concatenate([first, second], axis=0)
    return jnp.stack(pieces)


def ring_reduce_scatter(term, axis, n):
    if n == 1:
        return [term(0, True).astype(jnp.float32), term(0, False).astype(jnp.float32)]
    results = []
    for lower, direction in ((True, 1), (False, -1)):
        carried = term(-direction % n, lower)
        for step in range(1, n):
            arrived = shift(carried, axis, n, direction)
            own = term((-direction * (step + 1)) % n, lower)
            total = arrived.astype(jnp.float32) + own.astype(jnp.float32)
            carried = total.astype(own.dtype) if step < n - 1 else total
        results.append(carried)
    return results


def shards(
    tokens, norm_gain, router_weight, gate_proj, up_proj, down_proj, expert_ids, slots, capacity
):
    tok_rows, shard_width = tokens.shape
    model_width = norm_gain.shape[0]
    experts = router_weight.shape[1]
    n_mp = model_width // shard_width
    slot_count = 4 * tok_rows // (3 * experts)
    cells = experts * slot_count
    me = lax.axis_index("expert")

    onehot = expert_ids[:, None] == jnp.arange(experts, dtype=jnp.int32)[None, :]
    cap_token = jnp.sum(jnp.where(onehot, capacity[None, :], 0), axis=1)
    kept_rows = slots < cap_token
    target = expert_ids * slot_count + slots
    route = (
        (target[:, None] == jnp.arange(cells, dtype=jnp.int32)[None, :]) & kept_rows[:, None]
    ).astype(jnp.bfloat16)

    masked = lax.dot_general(
        route, tokens, (((0,), (0,)), ((), ())), preferred_element_type=jnp.float32
    ).astype(jnp.bfloat16)
    n_z = lax.psum(1, "mz")
    n_x = n_mp // n_z
    groups = lax.psum(1, "expert")
    spread = jnp.broadcast_to(
        masked.reshape(experts, 1, slot_count, shard_width), (experts, n_z, slot_count, shard_width)
    )
    received = lax.all_to_all(
        spread.reshape(experts * n_z, slot_count, shard_width),
        ("expert", "mz"),
        split_axis=0,
        concat_axis=0,
        tiled=True,
    ).reshape(groups, n_z, slot_count, shard_width)
    at_x = lax.axis_index("mx")
    x_width = model_width // n_x

    def rows_relative(w):
        return jnp.roll(w, -at_x * x_width, axis=0)

    whole = ring_gather(received, "mx", n_x)
    features = jnp.transpose(whole, (1, 3, 0, 2, 4)).reshape(cells, model_width)
    features = features.astype(jnp.float32)
    mean_square = jnp.sum(features * features, axis=1) / model_width
    scale = lax.rsqrt(mean_square + norm_eps)
    normed = (features * scale[:, None] * rows_relative(norm_gain)).astype(jnp.bfloat16)

    logits = jnp.dot(normed, rows_relative(router_weight), preferred_element_type=jnp.float32)
    picked = jnp.sum(
        jnp.where(jnp.arange(experts, dtype=jnp.int32)[None, :] == me, logits, 0.0), axis=1
    )
    gate_prob = jax.nn.sigmoid(picked)

    pre_gate = jnp.dot(normed, rows_relative(gate_proj[0]), preferred_element_type=jnp.float32)
    pre_up = jnp.dot(normed, rows_relative(up_proj[0]), preferred_element_type=jnp.float32)
    hidden = (jax.nn.gelu(pre_gate, approximate=True) * pre_up).astype(jnp.bfloat16)
    rows_half = cells // 2
    hidden_halves = {True: hidden[:rows_half], False: hidden[rows_half:]}

    def x_term(k, lower):
        columns = lax.dynamic_slice_in_dim(
            down_proj[0], ((at_x + k) % n_x) * x_width, x_width, axis=1
        )
        return jnp.dot(hidden_halves[lower], columns, preferred_element_type=jnp.float32).astype(
            jnp.bfloat16
        )

    across_x = jnp.concatenate(ring_reduce_scatter(x_term, "mx", n_x), axis=0)
    gated = (gate_prob[:, None] * across_x).astype(jnp.bfloat16)
    gated = jnp.transpose(gated.reshape(groups, slot_count, n_z, shard_width), (0, 2, 1, 3))
    returned = lax.all_to_all(
        gated.reshape(groups * n_z, slot_count, shard_width),
        ("expert", "mz"),
        split_axis=0,
        concat_axis=0,
        tiled=True,
    ).reshape(experts, n_z, slot_count, shard_width)
    returned = jnp.sum(returned.astype(jnp.float32), axis=1).astype(jnp.bfloat16)
    update = jnp.dot(route, returned.reshape(cells, shard_width), preferred_element_type=jnp.float32)
    return update.astype(jnp.bfloat16)


def solution(mesh):
    n_expert, n_mp = mesh.devices.shape
    n_x = len({device.coords[0] for device in mesh.devices[0]})
    split = Mesh(mesh.devices.reshape(n_expert, n_x, n_mp // n_x), ("expert", "mx", "mz"))
    mp = ("mx", "mz")
    in_specs = (
        P("expert", mp),
        P(),
        P(),
        P("expert", None, mp),
        P("expert", None, mp),
        P("expert", mp, None),
        P("expert"),
        P("expert"),
        P(),
    )
    out_specs = P("expert", mp)
    return jax.shard_map(shards, mesh=split, in_specs=in_specs, out_specs=out_specs, check_vma=False)
```

```python
import jax
import jax.numpy as jnp
from jax import lax
from jax.sharding import Mesh, PartitionSpec as P

norm_eps = 1e-06


def shift(value, axis, n, step):
    return lax.ppermute(value, axis, [(i, (i + step) % n) for i in range(n)])


def ring_gather(block, axis, n):
    if n == 1:
        return block[None]
    half = block.shape[0] // 2
    pieces = [None] * n
    pieces[0] = block
    rightward = leftward = block
    for step in range(1, (n + 1) // 2):
        rightward = shift(rightward, axis, n, 1)
        leftward = shift(leftward, axis, n, -1)
        pieces[n - step] = rightward
        pieces[step] = leftward
    if n % 2 == 0:
        first = shift(rightward[:half], axis, n, 1)
        second = shift(leftward[half:], axis, n, -1)
        pieces[n // 2] = jnp.concatenate([first, second], axis=0)
    return jnp.stack(pieces)


def ring_reduce_scatter(term, axis, n):
    if n == 1:
        return [term(0, True).astype(jnp.float32), term(0, False).astype(jnp.float32)]
    results = []
    for lower, direction in ((True, 1), (False, -1)):
        carried = term(-direction % n, lower)
        for step in range(1, n):
            arrived = shift(carried, axis, n, direction)
            own = term((-direction * (step + 1)) % n, lower)
            total = arrived.astype(jnp.float32) + own.astype(jnp.float32)
            carried = total.astype(own.dtype) if step < n - 1 else total
        results.append(carried)
    return results


def shards(
    tokens, norm_gain, router_weight, gate_proj, up_proj, down_proj, expert_ids, slots, capacity
):
    tok_rows, shard_width = tokens.shape
    model_width = norm_gain.shape[0]
    experts = router_weight.shape[1]
    n_mp = model_width // shard_width
    slot_count = 4 * tok_rows // (3 * experts)
    cells = experts * slot_count
    me = lax.axis_index("expert")

    onehot = expert_ids[:, None] == jnp.arange(experts, dtype=jnp.int32)[None, :]
    cap_token = jnp.sum(jnp.where(onehot, capacity[None, :], 0), axis=1)
    kept_rows = slots < cap_token
    target = expert_ids * slot_count + slots
    route = (
        (target[:, None] == jnp.arange(cells, dtype=jnp.int32)[None, :]) & kept_rows[:, None]
    ).astype(jnp.bfloat16)

    masked = lax.dot_general(
        route, tokens, (((0,), (0,)), ((), ())), preferred_element_type=jnp.float32
    ).astype(jnp.bfloat16)
    received = lax.all_to_all(
        masked.reshape(experts, slot_count, shard_width),
        "expert",
        split_axis=0,
        concat_axis=0,
        tiled=True,
    ).reshape(cells, shard_width)
    n_z = lax.psum(1, "mz")
    n_x = n_mp // n_z
    at_x = lax.axis_index("mx")
    x_width = model_width // n_x

    def rows_relative(w):
        return jnp.roll(w, -at_x * x_width, axis=0)

    copies = jnp.broadcast_to(received[None], (n_z, cells, shard_width))
    part = lax.all_to_all(copies, "mz", split_axis=0, concat_axis=0, tiled=True)
    whole = ring_gather(part, "mx", n_x).reshape(n_mp, cells, shard_width)

    features = jnp.transpose(whole, (1, 0, 2)).reshape(cells, model_width).astype(jnp.float32)
    mean_square = jnp.sum(features * features, axis=1) / model_width
    scale = lax.rsqrt(mean_square + norm_eps)
    normed = (features * scale[:, None] * rows_relative(norm_gain)).astype(jnp.bfloat16)

    logits = jnp.dot(normed, rows_relative(router_weight), preferred_element_type=jnp.float32)
    picked = jnp.sum(
        jnp.where(jnp.arange(experts, dtype=jnp.int32)[None, :] == me, logits, 0.0), axis=1
    )
    gate_prob = jax.nn.sigmoid(picked)

    ff_local = gate_proj.shape[2]
    pre_gate = jnp.dot(normed, rows_relative(gate_proj[0]), preferred_element_type=jnp.float32)
    pre_up = jnp.dot(normed, rows_relative(up_proj[0]), preferred_element_type=jnp.float32)
    hidden = (jax.nn.gelu(pre_gate, approximate=True) * pre_up).astype(jnp.bfloat16)
    rows_half = cells // 2
    hidden_halves = {True: hidden[:rows_half], False: hidden[rows_half:]}

    def x_term(k, lower):
        columns = lax.dynamic_slice_in_dim(
            down_proj[0], ((at_x + k) % n_x) * x_width, x_width, axis=1
        )
        return jnp.dot(hidden_halves[lower], columns, preferred_element_type=jnp.float32).astype(
            jnp.bfloat16
        )

    across_x = [part.astype(jnp.bfloat16) for part in ring_reduce_scatter(x_term, "mx", n_x)]

    across_x = jnp.concatenate(across_x, axis=0).reshape(cells, n_z, shard_width)
    z_terms = lax.all_to_all(
        jnp.transpose(across_x, (1, 0, 2)), "mz", split_axis=0, concat_axis=0, tiled=True
    )
    summed = jnp.sum(z_terms.astype(jnp.float32), axis=0).astype(jnp.bfloat16)
    gated = (gate_prob[:, None] * summed.astype(jnp.float32)).astype(jnp.bfloat16)

    returned = lax.all_to_all(
        gated.reshape(experts, slot_count, shard_width),
        "expert",
        split_axis=0,
        concat_axis=0,
        tiled=True,
    ).reshape(cells, shard_width)
    update = jnp.dot(route, returned, preferred_element_type=jnp.float32)
    return update.astype(jnp.bfloat16)


def solution(mesh):
    n_expert, n_mp = mesh.devices.shape
    n_x = len({device.coords[0] for device in mesh.devices[0]})
    split = Mesh(mesh.devices.reshape(n_expert, n_x, n_mp // n_x), ("expert", "mx", "mz"))
    mp = ("mx", "mz")
    in_specs = (
        P("expert", mp),
        P(),
        P(),
        P("expert", None, mp),
        P("expert", None, mp),
        P("expert", mp, None),
        P("expert"),
        P("expert"),
        P(),
    )
    out_specs = P("expert", mp)
    return jax.shard_map(shards, mesh=split, in_specs=in_specs, out_specs=out_specs, check_vma=False)
```

```python
import jax
import jax.numpy as jnp
from jax import lax
from jax.sharding import Mesh, PartitionSpec as P

norm_eps = 1e-06


def shift(value, axis, n, step):
    return lax.ppermute(value, axis, [(i, (i + step) % n) for i in range(n)])


def ring_gather(block, axis, n):
    if n == 1:
        return block[None]
    half = block.shape[0] // 2
    pieces = [None] * n
    pieces[0] = block
    rightward = leftward = block
    for step in range(1, (n + 1) // 2):
        rightward = shift(rightward, axis, n, 1)
        leftward = shift(leftward, axis, n, -1)
        pieces[n - step] = rightward
        pieces[step] = leftward
    if n % 2 == 0:
        first = shift(rightward[:half], axis, n, 1)
        second = shift(leftward[half:], axis, n, -1)
        pieces[n // 2] = jnp.concatenate([first, second], axis=0)
    return jnp.stack(pieces)


def ring_reduce_scatter(term, axis, n):
    if n == 1:
        return [term(0, True).astype(jnp.float32), term(0, False).astype(jnp.float32)]
    results = []
    for lower, direction in ((True, 1), (False, -1)):
        carried = term(-direction % n, lower)
        for step in range(1, n):
            arrived = shift(carried, axis, n, direction)
            own = term((-direction * (step + 1)) % n, lower)
            total = arrived.astype(jnp.float32) + own.astype(jnp.float32)
            carried = total.astype(own.dtype) if step < n - 1 else total
        results.append(carried)
    return results


def shards(
    tokens, norm_gain, router_weight, gate_proj, up_proj, down_proj, expert_ids, slots, capacity
):
    tok_rows, shard_width = tokens.shape
    model_width = norm_gain.shape[0]
    experts = router_weight.shape[1]
    n_mp = model_width // shard_width
    slot_count = 4 * tok_rows // (3 * experts)
    cells = experts * slot_count
    me = lax.axis_index("expert")

    onehot = expert_ids[:, None] == jnp.arange(experts, dtype=jnp.int32)[None, :]
    cap_token = jnp.sum(jnp.where(onehot, capacity[None, :], 0), axis=1)
    kept_rows = slots < cap_token
    target = expert_ids * slot_count + slots
    route = (
        (target[:, None] == jnp.arange(cells, dtype=jnp.int32)[None, :]) & kept_rows[:, None]
    ).astype(jnp.bfloat16)

    masked = lax.dot_general(
        route, tokens, (((0,), (0,)), ((), ())), preferred_element_type=jnp.float32
    ).astype(jnp.bfloat16)
    n_z = lax.psum(1, "mz")
    n_x = n_mp // n_z
    at_x = lax.axis_index("mx")
    x_width = model_width // n_x

    def rows_relative(w):
        return jnp.roll(w, -at_x * x_width, axis=0)

    copies = jnp.broadcast_to(masked[None], (n_z, cells, shard_width))
    part = lax.all_to_all(
        copies.reshape(n_z * experts, slot_count, shard_width),
        ("mz", "expert"),
        split_axis=0,
        concat_axis=0,
        tiled=True,
    ).reshape(n_z, cells, shard_width)
    whole = ring_gather(part, "mx", n_x).reshape(n_mp, cells, shard_width)

    features = jnp.transpose(whole, (1, 0, 2)).reshape(cells, model_width).astype(jnp.float32)
    mean_square = jnp.sum(features * features, axis=1) / model_width
    scale = lax.rsqrt(mean_square + norm_eps)
    normed = (features * scale[:, None] * rows_relative(norm_gain)).astype(jnp.bfloat16)

    logits = jnp.dot(normed, rows_relative(router_weight), preferred_element_type=jnp.float32)
    picked = jnp.sum(
        jnp.where(jnp.arange(experts, dtype=jnp.int32)[None, :] == me, logits, 0.0), axis=1
    )
    gate_prob = jax.nn.sigmoid(picked)

    ff_local = gate_proj.shape[2]
    pre_gate = jnp.dot(normed, rows_relative(gate_proj[0]), preferred_element_type=jnp.float32)
    pre_up = jnp.dot(normed, rows_relative(up_proj[0]), preferred_element_type=jnp.float32)
    hidden = (jax.nn.gelu(pre_gate, approximate=True) * pre_up).astype(jnp.bfloat16)
    rows_half = cells // 2
    hidden_halves = {True: hidden[:rows_half], False: hidden[rows_half:]}

    def x_term(k, lower):
        columns = lax.dynamic_slice_in_dim(
            down_proj[0], ((at_x + k) % n_x) * x_width, x_width, axis=1
        )
        return jnp.dot(hidden_halves[lower], columns, preferred_element_type=jnp.float32).astype(
            jnp.bfloat16
        )

    across_x = [part.astype(jnp.bfloat16) for part in ring_reduce_scatter(x_term, "mx", n_x)]

    across_x = jnp.concatenate(across_x, axis=0).reshape(cells, n_z, shard_width)
    z_terms = lax.all_to_all(
        jnp.transpose(across_x, (1, 0, 2)), "mz", split_axis=0, concat_axis=0, tiled=True
    )
    summed = jnp.sum(z_terms.astype(jnp.float32), axis=0).astype(jnp.bfloat16)
    gated = (gate_prob[:, None] * summed.astype(jnp.float32)).astype(jnp.bfloat16)

    returned = lax.all_to_all(
        gated.reshape(experts, slot_count, shard_width),
        "expert",
        split_axis=0,
        concat_axis=0,
        tiled=True,
    ).reshape(cells, shard_width)
    update = jnp.dot(route, returned, preferred_element_type=jnp.float32)
    return update.astype(jnp.bfloat16)


def solution(mesh):
    n_expert, n_mp = mesh.devices.shape
    n_x = len({device.coords[0] for device in mesh.devices[0]})
    split = Mesh(mesh.devices.reshape(n_expert, n_x, n_mp // n_x), ("expert", "mx", "mz"))
    mp = ("mx", "mz")
    in_specs = (
        P("expert", mp),
        P(),
        P(),
        P("expert", None, mp),
        P("expert", None, mp),
        P("expert", mp, None),
        P("expert"),
        P("expert"),
        P(),
    )
    out_specs = P("expert", mp)
    return jax.shard_map(shards, mesh=split, in_specs=in_specs, out_specs=out_specs, check_vma=False)
```

```python
import jax
import jax.numpy as jnp
from jax import lax
from jax.sharding import Mesh, PartitionSpec as P

norm_eps = 1e-06


def shift(value, axis, n, step):
    return lax.ppermute(value, axis, [(i, (i + step) % n) for i in range(n)])


def ring_gather(block, axis, n):
    if n == 1:
        return [block]
    half = block.shape[0] // 2
    pieces = [None] * n
    pieces[0] = block
    rightward = leftward = block
    for step in range(1, (n + 1) // 2):
        rightward = shift(rightward, axis, n, 1)
        leftward = shift(leftward, axis, n, -1)
        pieces[n - step] = rightward
        pieces[step] = leftward
    if n % 2 == 0:
        first = shift(rightward[:half], axis, n, 1)
        second = shift(leftward[half:], axis, n, -1)
        pieces[n // 2] = jnp.concatenate([first, second], axis=0)
    return pieces


def ring_reduce_scatter(term, axis, n):
    if n == 1:
        return [term(0, True).astype(jnp.float32), term(0, False).astype(jnp.float32)]
    results = []
    for lower, direction in ((True, 1), (False, -1)):
        carried = term(-direction % n, lower)
        for step in range(1, n):
            arrived = shift(carried, axis, n, direction)
            own = term((-direction * (step + 1)) % n, lower)
            total = arrived.astype(jnp.float32) + own.astype(jnp.float32)
            carried = total.astype(own.dtype) if step < n - 1 else total
        results.append(carried)
    return results


def shards(
    tokens, norm_gain, router_weight, gate_proj, up_proj, down_proj, expert_ids, slots, capacity
):
    tok_rows, shard_width = tokens.shape
    model_width = norm_gain.shape[0]
    experts = router_weight.shape[1]
    n_mp = model_width // shard_width
    slot_count = 4 * tok_rows // (3 * experts)
    cells = experts * slot_count
    me = lax.axis_index("expert")

    onehot = expert_ids[:, None] == jnp.arange(experts, dtype=jnp.int32)[None, :]
    cap_token = jnp.sum(jnp.where(onehot, capacity[None, :], 0), axis=1)
    kept_rows = slots < cap_token
    target = expert_ids * slot_count + slots
    route = (
        (target[:, None] == jnp.arange(cells, dtype=jnp.int32)[None, :]) & kept_rows[:, None]
    ).astype(jnp.bfloat16)

    masked = lax.dot_general(
        route, tokens, (((0,), (0,)), ((), ())), preferred_element_type=jnp.float32
    ).astype(jnp.bfloat16)
    n_z = lax.psum(1, "mz")
    n_x = n_mp // n_z
    at_x = lax.axis_index("mx")
    x_width = model_width // n_x

    def rows_relative(w):
        return jnp.roll(w, -at_x * x_width, axis=0)

    copies = jnp.broadcast_to(masked[None], (n_z, cells, shard_width))
    part = lax.all_to_all(
        copies.reshape(n_z * experts, slot_count, shard_width),
        ("mz", "expert"),
        split_axis=0,
        concat_axis=0,
        tiled=True,
    ).reshape(n_z, cells, shard_width)
    part = jnp.swapaxes(part, 1, 2)
    blocks = [block.reshape(x_width, cells) for block in ring_gather(part, "mx", n_x)]
    mean_square = sum(
        jnp.sum(jnp.square(block.astype(jnp.float32)), axis=0) for block in blocks
    ) / model_width
    scale = lax.rsqrt(mean_square + norm_eps)
    gain = rows_relative(norm_gain)
    normed = [
        (block.astype(jnp.float32) * scale[None, :] * gain[k * x_width : (k + 1) * x_width, None])
        .astype(jnp.bfloat16)
        for k, block in enumerate(blocks)
    ]
    by_feature = (((0,), (0,)), ((), ()))

    def project(w):
        w = rows_relative(w)
        return sum(
            lax.dot_general(
                block,
                w[k * x_width : (k + 1) * x_width],
                by_feature,
                preferred_element_type=jnp.float32,
            )
            for k, block in enumerate(normed)
        )

    logits = project(router_weight)
    picked = jnp.sum(
        jnp.where(jnp.arange(experts, dtype=jnp.int32)[None, :] == me, logits, 0.0), axis=1
    )
    gate_prob = jax.nn.sigmoid(picked)

    ff_local = gate_proj.shape[2]
    pre_gate = project(gate_proj[0])
    pre_up = project(up_proj[0])
    hidden = (jax.nn.gelu(pre_gate, approximate=True) * pre_up).astype(jnp.bfloat16)
    rows_half = cells // 2
    hidden_halves = {True: hidden[:rows_half], False: hidden[rows_half:]}

    def x_term(k, lower):
        columns = lax.dynamic_slice_in_dim(
            down_proj[0], ((at_x + k) % n_x) * x_width, x_width, axis=1
        )
        return jnp.dot(hidden_halves[lower], columns, preferred_element_type=jnp.float32).astype(
            jnp.bfloat16
        )

    across_x = [part.astype(jnp.bfloat16) for part in ring_reduce_scatter(x_term, "mx", n_x)]

    across_x = jnp.concatenate(across_x, axis=0).reshape(cells, n_z, shard_width)
    z_terms = lax.all_to_all(
        jnp.transpose(across_x, (1, 0, 2)), "mz", split_axis=0, concat_axis=0, tiled=True
    )
    summed = jnp.sum(z_terms.astype(jnp.float32), axis=0).astype(jnp.bfloat16)
    gated = (gate_prob[:, None] * summed.astype(jnp.float32)).astype(jnp.bfloat16)

    returned = lax.all_to_all(
        gated.reshape(experts, slot_count, shard_width),
        "expert",
        split_axis=0,
        concat_axis=0,
        tiled=True,
    ).reshape(cells, shard_width)
    update = jnp.dot(route, returned, preferred_element_type=jnp.float32)
    return update.astype(jnp.bfloat16)


def solution(mesh):
    n_expert, n_mp = mesh.devices.shape
    n_x = len({device.coords[0] for device in mesh.devices[0]})
    split = Mesh(mesh.devices.reshape(n_expert, n_x, n_mp // n_x), ("expert", "mx", "mz"))
    mp = ("mx", "mz")
    in_specs = (
        P("expert", mp),
        P(),
        P(),
        P("expert", None, mp),
        P("expert", None, mp),
        P("expert", mp, None),
        P("expert"),
        P("expert"),
        P(),
    )
    out_specs = P("expert", mp)
    return jax.shard_map(shards, mesh=split, in_specs=in_specs, out_specs=out_specs, check_vma=False)
```

```python
import jax
import jax.numpy as jnp
from jax import lax
from jax.sharding import Mesh, PartitionSpec as P

norm_eps = 1e-06


def shift(value, axis, n, step):
    return lax.ppermute(value, axis, [(i, (i + step) % n) for i in range(n)])


def ring_gather(block, axis, n):
    if n == 1:
        return block[None]
    half = block.shape[0] // 2
    pieces = [None] * n
    pieces[0] = block
    rightward = leftward = block
    for step in range(1, (n + 1) // 2):
        rightward = shift(rightward, axis, n, 1)
        leftward = shift(leftward, axis, n, -1)
        pieces[n - step] = rightward
        pieces[step] = leftward
    if n % 2 == 0:
        first = shift(rightward[:half], axis, n, 1)
        second = shift(leftward[half:], axis, n, -1)
        pieces[n // 2] = jnp.concatenate([first, second], axis=0)
    return jnp.stack(pieces)


def ring_reduce_scatter(term, axis, n):
    if n == 1:
        return [term(0, True).astype(jnp.float32), term(0, False).astype(jnp.float32)]
    results = []
    for lower, direction in ((True, 1), (False, -1)):
        carried = term(-direction % n, lower)
        for step in range(1, n):
            arrived = shift(carried, axis, n, direction)
            own = term((-direction * (step + 1)) % n, lower)
            total = arrived.astype(jnp.float32) + own.astype(jnp.float32)
            carried = total.astype(own.dtype) if step < n - 1 else total
        results.append(carried)
    return results


def shards(
    tokens, norm_gain, router_weight, gate_proj, up_proj, down_proj, expert_ids, slots, capacity
):
    tok_rows, shard_width = tokens.shape
    model_width = norm_gain.shape[0]
    experts = router_weight.shape[1]
    n_mp = model_width // shard_width
    slot_count = 4 * tok_rows // (3 * experts)
    cells = experts * slot_count
    me = lax.axis_index("expert")

    onehot = expert_ids[:, None] == jnp.arange(experts, dtype=jnp.int32)[None, :]
    cap_token = jnp.sum(jnp.where(onehot, capacity[None, :], 0), axis=1)
    kept_rows = slots < cap_token
    target = expert_ids * slot_count + slots
    route = (
        (target[:, None] == jnp.arange(cells, dtype=jnp.int32)[None, :]) & kept_rows[:, None]
    ).astype(jnp.bfloat16)

    masked = lax.dot_general(
        route, tokens, (((0,), (0,)), ((), ())), preferred_element_type=jnp.float32
    ).astype(jnp.bfloat16)
    received = lax.all_to_all(
        masked.reshape(experts, slot_count, shard_width),
        "expert",
        split_axis=0,
        concat_axis=0,
        tiled=True,
    ).reshape(cells, shard_width)
    n_z = lax.psum(1, "mz")
    n_x = n_mp // n_z
    at_x = lax.axis_index("mx")
    x_width = model_width // n_x

    def rows_relative(w):
        return jnp.roll(w, -at_x * x_width, axis=0)

    halves = []
    for rows in (received[: cells // 2], received[cells // 2 :]):
        copies = jnp.broadcast_to(rows[None], (n_z,) + rows.shape)
        part = lax.all_to_all(copies, "mz", split_axis=0, concat_axis=0, tiled=True)
        halves.append(ring_gather(part, "mx", n_x).reshape(n_mp, cells // 2, shard_width))
    whole = jnp.concatenate(halves, axis=1)

    features = jnp.transpose(whole, (1, 0, 2)).reshape(cells, model_width).astype(jnp.float32)
    mean_square = jnp.sum(features * features, axis=1) / model_width
    scale = lax.rsqrt(mean_square + norm_eps)
    normed = (features * scale[:, None] * rows_relative(norm_gain)).astype(jnp.bfloat16)

    logits = jnp.dot(normed, rows_relative(router_weight), preferred_element_type=jnp.float32)
    picked = jnp.sum(
        jnp.where(jnp.arange(experts, dtype=jnp.int32)[None, :] == me, logits, 0.0), axis=1
    )
    gate_prob = jax.nn.sigmoid(picked)

    ff_local = gate_proj.shape[2]
    pre_gate = jnp.dot(normed, rows_relative(gate_proj[0]), preferred_element_type=jnp.float32)
    pre_up = jnp.dot(normed, rows_relative(up_proj[0]), preferred_element_type=jnp.float32)
    hidden = (jax.nn.gelu(pre_gate, approximate=True) * pre_up).astype(jnp.bfloat16)
    rows_half = cells // 2
    hidden_halves = {True: hidden[:rows_half], False: hidden[rows_half:]}

    def x_term(k, lower):
        columns = lax.dynamic_slice_in_dim(
            down_proj[0], ((at_x + k) % n_x) * x_width, x_width, axis=1
        )
        return jnp.dot(hidden_halves[lower], columns, preferred_element_type=jnp.float32).astype(
            jnp.bfloat16
        )

    across_x = [part.astype(jnp.bfloat16) for part in ring_reduce_scatter(x_term, "mx", n_x)]

    across_x = jnp.concatenate(across_x, axis=0).reshape(cells, n_z, shard_width)
    z_terms = lax.all_to_all(
        jnp.transpose(across_x, (1, 0, 2)), "mz", split_axis=0, concat_axis=0, tiled=True
    )
    summed = jnp.sum(z_terms.astype(jnp.float32), axis=0).astype(jnp.bfloat16)
    gated = (gate_prob[:, None] * summed.astype(jnp.float32)).astype(jnp.bfloat16)

    returned = lax.all_to_all(
        gated.reshape(experts, slot_count, shard_width),
        "expert",
        split_axis=0,
        concat_axis=0,
        tiled=True,
    ).reshape(cells, shard_width)
    update = jnp.dot(route, returned, preferred_element_type=jnp.float32)
    return update.astype(jnp.bfloat16)


def solution(mesh):
    n_expert, n_mp = mesh.devices.shape
    n_x = len({device.coords[0] for device in mesh.devices[0]})
    split = Mesh(mesh.devices.reshape(n_expert, n_x, n_mp // n_x), ("expert", "mx", "mz"))
    mp = ("mx", "mz")
    in_specs = (
        P("expert", mp),
        P(),
        P(),
        P("expert", None, mp),
        P("expert", None, mp),
        P("expert", mp, None),
        P("expert"),
        P("expert"),
        P(),
    )
    out_specs = P("expert", mp)
    return jax.shard_map(shards, mesh=split, in_specs=in_specs, out_specs=out_specs, check_vma=False)
```

```python
import jax
import jax.numpy as jnp
from jax import lax
from jax.sharding import Mesh, PartitionSpec as P

norm_eps = 1e-06


def shift(value, axis, n, step):
    return lax.ppermute(value, axis, [(i, (i + step) % n) for i in range(n)])


def ring_gather(block, axis, n):
    if n == 1:
        return block[None]
    half = block.shape[0] // 2
    pieces = [None] * n
    pieces[0] = block
    rightward = leftward = block
    for step in range(1, (n + 1) // 2):
        rightward = shift(rightward, axis, n, 1)
        leftward = shift(leftward, axis, n, -1)
        pieces[n - step] = rightward
        pieces[step] = leftward
    if n % 2 == 0:
        first = shift(rightward[:half], axis, n, 1)
        second = shift(leftward[half:], axis, n, -1)
        pieces[n // 2] = jnp.concatenate([first, second], axis=0)
    return jnp.stack(pieces)


def ring_reduce_scatter(term, axis, n):
    if n == 1:
        return [term(0, True).astype(jnp.float32), term(0, False).astype(jnp.float32)]
    results = []
    for lower, direction in ((True, 1), (False, -1)):
        carried = term(-direction % n, lower)
        for step in range(1, n):
            arrived = shift(carried, axis, n, direction)
            own = term((-direction * (step + 1)) % n, lower)
            total = arrived.astype(jnp.float32) + own.astype(jnp.float32)
            carried = total.astype(own.dtype) if step < n - 1 else total
        results.append(carried)
    return results


def shards(
    tokens, norm_gain, router_weight, gate_proj, up_proj, down_proj, expert_ids, slots, capacity
):
    tok_rows, shard_width = tokens.shape
    model_width = norm_gain.shape[0]
    experts = router_weight.shape[1]
    n_mp = model_width // shard_width
    slot_count = 4 * tok_rows // (3 * experts)
    cells = experts * slot_count
    me = lax.axis_index("expert")

    onehot = expert_ids[:, None] == jnp.arange(experts, dtype=jnp.int32)[None, :]
    cap_token = jnp.sum(jnp.where(onehot, capacity[None, :], 0), axis=1)
    kept_rows = slots < cap_token
    target = expert_ids * slot_count + slots
    route = (
        (target[:, None] == jnp.arange(cells, dtype=jnp.int32)[None, :]) & kept_rows[:, None]
    ).astype(jnp.bfloat16)

    masked = lax.dot_general(
        route, tokens, (((0,), (0,)), ((), ())), preferred_element_type=jnp.float32
    ).astype(jnp.bfloat16)
    by_half = masked.reshape(experts, 2, slot_count // 2, shard_width)
    received = [
        lax.all_to_all(by_half[:, h], "expert", split_axis=0, concat_axis=0, tiled=True).reshape(
            cells // 2, shard_width
        )
        for h in range(2)
    ]
    n_z = lax.psum(1, "mz")
    n_x = n_mp // n_z
    at_x = lax.axis_index("mx")
    x_width = model_width // n_x

    def rows_relative(w):
        return jnp.roll(w, -at_x * x_width, axis=0)

    halves = []
    for rows in received:
        copies = jnp.broadcast_to(rows[None], (n_z,) + rows.shape)
        part = lax.all_to_all(copies, "mz", split_axis=0, concat_axis=0, tiled=True)
        halves.append(ring_gather(part, "mx", n_x).reshape(n_mp, cells // 2, shard_width))
    whole = jnp.concatenate(halves, axis=1)

    features = jnp.transpose(whole, (1, 0, 2)).reshape(cells, model_width).astype(jnp.float32)
    mean_square = jnp.sum(features * features, axis=1) / model_width
    scale = lax.rsqrt(mean_square + norm_eps)
    normed = (features * scale[:, None] * rows_relative(norm_gain)).astype(jnp.bfloat16)

    logits = jnp.dot(normed, rows_relative(router_weight), preferred_element_type=jnp.float32)
    picked = jnp.sum(
        jnp.where(jnp.arange(experts, dtype=jnp.int32)[None, :] == me, logits, 0.0), axis=1
    )
    gate_prob = jax.nn.sigmoid(picked)

    ff_local = gate_proj.shape[2]
    pre_gate = jnp.dot(normed, rows_relative(gate_proj[0]), preferred_element_type=jnp.float32)
    pre_up = jnp.dot(normed, rows_relative(up_proj[0]), preferred_element_type=jnp.float32)
    hidden = (jax.nn.gelu(pre_gate, approximate=True) * pre_up).astype(jnp.bfloat16)
    rows_half = cells // 2
    hidden_halves = {True: hidden[:rows_half], False: hidden[rows_half:]}

    def x_term(k, lower):
        columns = lax.dynamic_slice_in_dim(
            down_proj[0], ((at_x + k) % n_x) * x_width, x_width, axis=1
        )
        return jnp.dot(hidden_halves[lower], columns, preferred_element_type=jnp.float32).astype(
            jnp.bfloat16
        )

    across_x = [part.astype(jnp.bfloat16) for part in ring_reduce_scatter(x_term, "mx", n_x)]

    across_x = jnp.concatenate(across_x, axis=0).reshape(cells, n_z, shard_width)
    z_terms = lax.all_to_all(
        jnp.transpose(across_x, (1, 0, 2)), "mz", split_axis=0, concat_axis=0, tiled=True
    )
    summed = jnp.sum(z_terms.astype(jnp.float32), axis=0).astype(jnp.bfloat16)
    gated = (gate_prob[:, None] * summed.astype(jnp.float32)).astype(jnp.bfloat16)

    gated = jnp.swapaxes(gated.reshape(2, experts, slot_count // 2, shard_width), 0, 1)
    returned = lax.all_to_all(
        gated.reshape(experts, slot_count, shard_width),
        "expert",
        split_axis=0,
        concat_axis=0,
        tiled=True,
    ).reshape(cells, shard_width)
    update = jnp.dot(route, returned, preferred_element_type=jnp.float32)
    return update.astype(jnp.bfloat16)


def solution(mesh):
    n_expert, n_mp = mesh.devices.shape
    n_x = len({device.coords[0] for device in mesh.devices[0]})
    split = Mesh(mesh.devices.reshape(n_expert, n_x, n_mp // n_x), ("expert", "mx", "mz"))
    mp = ("mx", "mz")
    in_specs = (
        P("expert", mp),
        P(),
        P(),
        P("expert", None, mp),
        P("expert", None, mp),
        P("expert", mp, None),
        P("expert"),
        P("expert"),
        P(),
    )
    out_specs = P("expert", mp)
    return jax.shard_map(shards, mesh=split, in_specs=in_specs, out_specs=out_specs, check_vma=False)
```

```python
import jax
import jax.numpy as jnp
from jax import lax
from jax.sharding import Mesh, PartitionSpec as P

norm_eps = 1e-06


def shift(value, axis, n, step):
    return lax.ppermute(value, axis, [(i, (i + step) % n) for i in range(n)])


def ring_gather(block, axis, n):
    if n == 1:
        return block[None]
    half = block.shape[0] // 2
    pieces = [None] * n
    pieces[0] = block
    rightward = leftward = block
    for step in range(1, (n + 1) // 2):
        rightward = shift(rightward, axis, n, 1)
        leftward = shift(leftward, axis, n, -1)
        pieces[n - step] = rightward
        pieces[step] = leftward
    if n % 2 == 0:
        first = shift(rightward[:half], axis, n, 1)
        second = shift(leftward[half:], axis, n, -1)
        pieces[n // 2] = jnp.concatenate([first, second], axis=0)
    return jnp.stack(pieces)


def ring_reduce_scatter(term, axis, n):
    if n == 1:
        return [term(0, True).astype(jnp.float32), term(0, False).astype(jnp.float32)]
    results = []
    for lower, direction in ((True, 1), (False, -1)):
        carried = term(-direction % n, lower)
        for step in range(1, n):
            arrived = shift(carried, axis, n, direction)
            own = term((-direction * (step + 1)) % n, lower)
            total = arrived.astype(jnp.float32) + own.astype(jnp.float32)
            carried = total.astype(own.dtype) if step < n - 1 else total
        results.append(carried)
    return results


def shards(
    tokens, norm_gain, router_weight, gate_proj, up_proj, down_proj, expert_ids, slots, capacity
):
    tok_rows, shard_width = tokens.shape
    model_width = norm_gain.shape[0]
    experts = router_weight.shape[1]
    n_mp = model_width // shard_width
    slot_count = 4 * tok_rows // (3 * experts)
    cells = experts * slot_count
    me = lax.axis_index("expert")

    onehot = expert_ids[:, None] == jnp.arange(experts, dtype=jnp.int32)[None, :]
    cap_token = jnp.sum(jnp.where(onehot, capacity[None, :], 0), axis=1)
    kept_rows = slots < cap_token
    target = expert_ids * slot_count + slots
    route = (
        (target[:, None] == jnp.arange(cells, dtype=jnp.int32)[None, :]) & kept_rows[:, None]
    ).astype(jnp.bfloat16)

    masked = lax.dot_general(
        route, tokens, (((0,), (0,)), ((), ())), preferred_element_type=jnp.float32
    ).astype(jnp.bfloat16)
    received = lax.all_to_all(
        masked.reshape(experts, slot_count, shard_width),
        "expert",
        split_axis=0,
        concat_axis=0,
        tiled=True,
    ).reshape(cells, shard_width)
    n_z = lax.psum(1, "mz")
    n_x = n_mp // n_z
    at_x = lax.axis_index("mx")
    x_width = model_width // n_x

    def rows_relative(w):
        return jnp.roll(w, -at_x * x_width, axis=0)

    chunk = cells // 4
    halves = []
    for at in range(0, cells, chunk):
        rows = received[at : at + chunk]
        copies = jnp.broadcast_to(rows[None], (n_z,) + rows.shape)
        part = lax.all_to_all(copies, "mz", split_axis=0, concat_axis=0, tiled=True)
        halves.append(ring_gather(part, "mx", n_x).reshape(n_mp, chunk, shard_width))
    whole = jnp.concatenate(halves, axis=1)

    features = jnp.transpose(whole, (1, 0, 2)).reshape(cells, model_width).astype(jnp.float32)
    mean_square = jnp.sum(features * features, axis=1) / model_width
    scale = lax.rsqrt(mean_square + norm_eps)
    normed = (features * scale[:, None] * rows_relative(norm_gain)).astype(jnp.bfloat16)

    logits = jnp.dot(normed, rows_relative(router_weight), preferred_element_type=jnp.float32)
    picked = jnp.sum(
        jnp.where(jnp.arange(experts, dtype=jnp.int32)[None, :] == me, logits, 0.0), axis=1
    )
    gate_prob = jax.nn.sigmoid(picked)

    ff_local = gate_proj.shape[2]
    pre_gate = jnp.dot(normed, rows_relative(gate_proj[0]), preferred_element_type=jnp.float32)
    pre_up = jnp.dot(normed, rows_relative(up_proj[0]), preferred_element_type=jnp.float32)
    hidden = (jax.nn.gelu(pre_gate, approximate=True) * pre_up).astype(jnp.bfloat16)
    rows_half = cells // 2
    hidden_halves = {True: hidden[:rows_half], False: hidden[rows_half:]}

    def x_term(k, lower):
        columns = lax.dynamic_slice_in_dim(
            down_proj[0], ((at_x + k) % n_x) * x_width, x_width, axis=1
        )
        return jnp.dot(hidden_halves[lower], columns, preferred_element_type=jnp.float32).astype(
            jnp.bfloat16
        )

    across_x = [part.astype(jnp.bfloat16) for part in ring_reduce_scatter(x_term, "mx", n_x)]

    across_x = jnp.concatenate(across_x, axis=0).reshape(cells, n_z, shard_width)
    z_terms = lax.all_to_all(
        jnp.transpose(across_x, (1, 0, 2)), "mz", split_axis=0, concat_axis=0, tiled=True
    )
    summed = jnp.sum(z_terms.astype(jnp.float32), axis=0).astype(jnp.bfloat16)
    gated = (gate_prob[:, None] * summed.astype(jnp.float32)).astype(jnp.bfloat16)

    returned = lax.all_to_all(
        gated.reshape(experts, slot_count, shard_width),
        "expert",
        split_axis=0,
        concat_axis=0,
        tiled=True,
    ).reshape(cells, shard_width)
    update = jnp.dot(route, returned, preferred_element_type=jnp.float32)
    return update.astype(jnp.bfloat16)


def solution(mesh):
    n_expert, n_mp = mesh.devices.shape
    n_x = len({device.coords[0] for device in mesh.devices[0]})
    split = Mesh(mesh.devices.reshape(n_expert, n_x, n_mp // n_x), ("expert", "mx", "mz"))
    mp = ("mx", "mz")
    in_specs = (
        P("expert", mp),
        P(),
        P(),
        P("expert", None, mp),
        P("expert", None, mp),
        P("expert", mp, None),
        P("expert"),
        P("expert"),
        P(),
    )
    out_specs = P("expert", mp)
    return jax.shard_map(shards, mesh=split, in_specs=in_specs, out_specs=out_specs, check_vma=False)
```

```python
import jax
import jax.numpy as jnp
from jax import lax
from jax.sharding import Mesh, PartitionSpec as P

norm_eps = 1e-06


def shift(value, axis, n, step):
    return lax.ppermute(value, axis, [(i, (i + step) % n) for i in range(n)])


def ring_gather(block, axis, n):
    if n == 1:
        return block[None]
    half = block.shape[0] // 2
    pieces = [None] * n
    pieces[0] = block
    rightward = leftward = block
    for step in range(1, (n + 1) // 2):
        rightward = shift(rightward, axis, n, 1)
        leftward = shift(leftward, axis, n, -1)
        pieces[n - step] = rightward
        pieces[step] = leftward
    if n % 2 == 0:
        first = shift(rightward[:half], axis, n, 1)
        second = shift(leftward[half:], axis, n, -1)
        pieces[n // 2] = jnp.concatenate([first, second], axis=0)
    return jnp.stack(pieces)


def ring_reduce_scatter(term, axis, n):
    if n == 1:
        return [term(0, True).astype(jnp.float32), term(0, False).astype(jnp.float32)]
    results = []
    for lower, direction in ((True, 1), (False, -1)):
        carried = term(-direction % n, lower)
        for step in range(1, n):
            arrived = shift(carried, axis, n, direction)
            own = term((-direction * (step + 1)) % n, lower)
            total = arrived.astype(jnp.float32) + own.astype(jnp.float32)
            carried = total.astype(own.dtype) if step < n - 1 else total
        results.append(carried)
    return results


def shards(
    tokens, norm_gain, router_weight, gate_proj, up_proj, down_proj, expert_ids, slots, capacity
):
    tok_rows, shard_width = tokens.shape
    model_width = norm_gain.shape[0]
    experts = router_weight.shape[1]
    n_mp = model_width // shard_width
    slot_count = 4 * tok_rows // (3 * experts)
    cells = experts * slot_count
    me = lax.axis_index("expert")

    onehot = expert_ids[:, None] == jnp.arange(experts, dtype=jnp.int32)[None, :]
    cap_token = jnp.sum(jnp.where(onehot, capacity[None, :], 0), axis=1)
    kept_rows = slots < cap_token
    target = expert_ids * slot_count + slots
    route = (
        (target[:, None] == jnp.arange(cells, dtype=jnp.int32)[None, :]) & kept_rows[:, None]
    ).astype(jnp.bfloat16)

    masked = lax.dot_general(
        route, tokens, (((0,), (0,)), ((), ())), preferred_element_type=jnp.float32
    ).astype(jnp.bfloat16)
    received = lax.all_to_all(
        masked.reshape(experts, slot_count, shard_width),
        "expert",
        split_axis=0,
        concat_axis=0,
        tiled=True,
    ).reshape(cells, shard_width)
    n_z = lax.psum(1, "mz")
    n_x = n_mp // n_z
    at_x = lax.axis_index("mx")
    x_width = model_width // n_x

    def rows_relative(w):
        return jnp.roll(w, -at_x * x_width, axis=0)

    halves = []
    for rows in (received[: cells // 2], received[cells // 2 :]):
        copies = jnp.broadcast_to(rows[None], (n_z,) + rows.shape)
        part = lax.all_to_all(copies, "mz", split_axis=0, concat_axis=0, tiled=True)
        halves.append(ring_gather(part, "mx", n_x).reshape(n_mp, cells // 2, shard_width))
    whole = jnp.concatenate(halves, axis=1)

    features = jnp.transpose(whole, (1, 0, 2)).reshape(cells, model_width).astype(jnp.float32)
    mean_square = jnp.sum(features * features, axis=1) / model_width
    scale = lax.rsqrt(mean_square + norm_eps)
    normed = (features * scale[:, None] * rows_relative(norm_gain)).astype(jnp.bfloat16)

    logits = jnp.dot(normed, rows_relative(router_weight), preferred_element_type=jnp.float32)
    picked = jnp.sum(
        jnp.where(jnp.arange(experts, dtype=jnp.int32)[None, :] == me, logits, 0.0), axis=1
    )
    gate_prob = jax.nn.sigmoid(picked)

    ff_local = gate_proj.shape[2]
    pre_gate = jnp.dot(normed, rows_relative(gate_proj[0]), preferred_element_type=jnp.float32)
    pre_up = jnp.dot(normed, rows_relative(up_proj[0]), preferred_element_type=jnp.float32)
    hidden = (jax.nn.gelu(pre_gate, approximate=True) * pre_up).astype(jnp.bfloat16)
    rows_half = cells // 2
    hidden_halves = {True: hidden[:rows_half], False: hidden[rows_half:]}

    def x_term(k, lower):
        columns = lax.dynamic_slice_in_dim(
            down_proj[0], ((at_x + k) % n_x) * x_width, x_width, axis=1
        )
        return jnp.dot(hidden_halves[lower], columns, preferred_element_type=jnp.float32).astype(
            jnp.bfloat16
        )

    summed = []
    for part in ring_reduce_scatter(x_term, "mx", n_x):
        part = part.astype(jnp.bfloat16).reshape(rows_half, n_z, shard_width)
        z_terms = lax.all_to_all(
            jnp.transpose(part, (1, 0, 2)), "mz", split_axis=0, concat_axis=0, tiled=True
        )
        summed.append(jnp.sum(z_terms.astype(jnp.float32), axis=0).astype(jnp.bfloat16))
    summed = jnp.concatenate(summed, axis=0)
    gated = (gate_prob[:, None] * summed.astype(jnp.float32)).astype(jnp.bfloat16)

    returned = lax.all_to_all(
        gated.reshape(experts, slot_count, shard_width),
        "expert",
        split_axis=0,
        concat_axis=0,
        tiled=True,
    ).reshape(cells, shard_width)
    update = jnp.dot(route, returned, preferred_element_type=jnp.float32)
    return update.astype(jnp.bfloat16)


def solution(mesh):
    n_expert, n_mp = mesh.devices.shape
    n_x = len({device.coords[0] for device in mesh.devices[0]})
    split = Mesh(mesh.devices.reshape(n_expert, n_x, n_mp // n_x), ("expert", "mx", "mz"))
    mp = ("mx", "mz")
    in_specs = (
        P("expert", mp),
        P(),
        P(),
        P("expert", None, mp),
        P("expert", None, mp),
        P("expert", mp, None),
        P("expert"),
        P("expert"),
        P(),
    )
    out_specs = P("expert", mp)
    return jax.shard_map(shards, mesh=split, in_specs=in_specs, out_specs=out_specs, check_vma=False)
```

```python
import jax
import jax.numpy as jnp
from jax import lax
from jax.sharding import Mesh, PartitionSpec as P

norm_eps = 1e-06


def shift(value, axis, n, step):
    return lax.ppermute(value, axis, [(i, (i + step) % n) for i in range(n)])


def ring_gather(block, axis, n):
    if n == 1:
        return block[None]
    half = block.shape[0] // 2
    pieces = [None] * n
    pieces[0] = block
    rightward = leftward = block
    for step in range(1, (n + 1) // 2):
        rightward = shift(rightward, axis, n, 1)
        leftward = shift(leftward, axis, n, -1)
        pieces[n - step] = rightward
        pieces[step] = leftward
    if n % 2 == 0:
        first = shift(rightward[:half], axis, n, 1)
        second = shift(leftward[half:], axis, n, -1)
        pieces[n // 2] = jnp.concatenate([first, second], axis=0)
    return jnp.stack(pieces)


def ring_reduce_scatter(term, axis, n):
    if n == 1:
        return [term(0, True).astype(jnp.float32), term(0, False).astype(jnp.float32)]
    results = []
    for lower, direction in ((True, 1), (False, -1)):
        carried = term(-direction % n, lower)
        for step in range(1, n):
            arrived = shift(carried, axis, n, direction)
            own = term((-direction * (step + 1)) % n, lower)
            total = arrived.astype(jnp.float32) + own.astype(jnp.float32)
            carried = total.astype(own.dtype) if step < n - 1 else total
        results.append(carried)
    return results


def shards(
    tokens, norm_gain, router_weight, gate_proj, up_proj, down_proj, expert_ids, slots, capacity
):
    tok_rows, shard_width = tokens.shape
    model_width = norm_gain.shape[0]
    experts = router_weight.shape[1]
    n_mp = model_width // shard_width
    slot_count = 4 * tok_rows // (3 * experts)
    cells = experts * slot_count
    me = lax.axis_index("expert")

    onehot = expert_ids[:, None] == jnp.arange(experts, dtype=jnp.int32)[None, :]
    cap_token = jnp.sum(jnp.where(onehot, capacity[None, :], 0), axis=1)
    kept_rows = slots < cap_token
    target = expert_ids * slot_count + slots
    route = (
        (target[:, None] == jnp.arange(cells, dtype=jnp.int32)[None, :]) & kept_rows[:, None]
    ).astype(jnp.bfloat16)

    masked = lax.dot_general(
        route, tokens, (((0,), (0,)), ((), ())), preferred_element_type=jnp.float32
    ).astype(jnp.bfloat16)
    received = lax.all_to_all(
        masked.reshape(experts, slot_count, shard_width),
        "expert",
        split_axis=0,
        concat_axis=0,
        tiled=True,
    ).reshape(cells, shard_width)
    n_z = lax.psum(1, "mz")
    n_x = n_mp // n_z
    at_x = lax.axis_index("mx")
    x_width = model_width // n_x

    def rows_relative(w):
        return jnp.roll(w, -at_x * x_width, axis=0)

    halves = []
    for rows in (received[: cells // 2], received[cells // 2 :]):
        copies = jnp.broadcast_to(rows[None], (n_z,) + rows.shape)
        part = lax.all_to_all(copies, "mz", split_axis=0, concat_axis=0, tiled=True)
        halves.append(ring_gather(part, "mx", n_x).reshape(n_mp, cells // 2, shard_width))
    hidden_halves = {}
    gate_parts = []
    for lower, whole in zip((True, False), halves):
        rows_half = whole.shape[1]
        features = jnp.transpose(whole, (1, 0, 2)).reshape(rows_half, model_width)
        features = features.astype(jnp.float32)
        mean_square = jnp.sum(features * features, axis=1) / model_width
        scale = lax.rsqrt(mean_square + norm_eps)
        normed = (features * scale[:, None] * rows_relative(norm_gain)).astype(jnp.bfloat16)

        logits = jnp.dot(normed, rows_relative(router_weight), preferred_element_type=jnp.float32)
        picked = jnp.sum(
            jnp.where(jnp.arange(experts, dtype=jnp.int32)[None, :] == me, logits, 0.0), axis=1
        )
        gate_parts.append(jax.nn.sigmoid(picked))

        pre_gate = jnp.dot(normed, rows_relative(gate_proj[0]), preferred_element_type=jnp.float32)
        pre_up = jnp.dot(normed, rows_relative(up_proj[0]), preferred_element_type=jnp.float32)
        hidden_halves[lower] = (jax.nn.gelu(pre_gate, approximate=True) * pre_up).astype(
            jnp.bfloat16
        )
    gate_prob = jnp.concatenate(gate_parts)

    def x_term(k, lower):
        columns = lax.dynamic_slice_in_dim(
            down_proj[0], ((at_x + k) % n_x) * x_width, x_width, axis=1
        )
        return jnp.dot(hidden_halves[lower], columns, preferred_element_type=jnp.float32).astype(
            jnp.bfloat16
        )

    across_x = [part.astype(jnp.bfloat16) for part in ring_reduce_scatter(x_term, "mx", n_x)]

    across_x = jnp.concatenate(across_x, axis=0).reshape(cells, n_z, shard_width)
    z_terms = lax.all_to_all(
        jnp.transpose(across_x, (1, 0, 2)), "mz", split_axis=0, concat_axis=0, tiled=True
    )
    summed = jnp.sum(z_terms.astype(jnp.float32), axis=0).astype(jnp.bfloat16)
    gated = (gate_prob[:, None] * summed.astype(jnp.float32)).astype(jnp.bfloat16)

    returned = lax.all_to_all(
        gated.reshape(experts, slot_count, shard_width),
        "expert",
        split_axis=0,
        concat_axis=0,
        tiled=True,
    ).reshape(cells, shard_width)
    update = jnp.dot(route, returned, preferred_element_type=jnp.float32)
    return update.astype(jnp.bfloat16)


def solution(mesh):
    n_expert, n_mp = mesh.devices.shape
    n_x = len({device.coords[0] for device in mesh.devices[0]})
    split = Mesh(mesh.devices.reshape(n_expert, n_x, n_mp // n_x), ("expert", "mx", "mz"))
    mp = ("mx", "mz")
    in_specs = (
        P("expert", mp),
        P(),
        P(),
        P("expert", None, mp),
        P("expert", None, mp),
        P("expert", mp, None),
        P("expert"),
        P("expert"),
        P(),
    )
    out_specs = P("expert", mp)
    return jax.shard_map(shards, mesh=split, in_specs=in_specs, out_specs=out_specs, check_vma=False)
```

```python
import jax
import jax.numpy as jnp
from jax import lax
from jax.sharding import Mesh, PartitionSpec as P

norm_eps = 1e-06


def shift(value, axis, n, step):
    return lax.ppermute(value, axis, [(i, (i + step) % n) for i in range(n)])


def ring_gather(block, axis, n):
    if n == 1:
        return block[None]
    half = block.shape[0] // 2
    pieces = [None] * n
    pieces[0] = block
    rightward = leftward = block
    for step in range(1, (n + 1) // 2):
        rightward = shift(rightward, axis, n, 1)
        leftward = shift(leftward, axis, n, -1)
        pieces[n - step] = rightward
        pieces[step] = leftward
    if n % 2 == 0:
        first = shift(rightward[:half], axis, n, 1)
        second = shift(leftward[half:], axis, n, -1)
        pieces[n // 2] = jnp.concatenate([first, second], axis=0)
    return jnp.stack(pieces)


def ring_reduce_scatter(term, axis, n):
    if n == 1:
        return [term(0, True).astype(jnp.float32), term(0, False).astype(jnp.float32)]
    results = []
    for lower, direction in ((True, 1), (False, -1)):
        carried = term(-direction % n, lower)
        for step in range(1, n):
            arrived = shift(carried, axis, n, direction)
            own = term((-direction * (step + 1)) % n, lower)
            total = arrived.astype(jnp.float32) + own.astype(jnp.float32)
            carried = total.astype(own.dtype) if step < n - 1 else total
        results.append(carried)
    return results


def shards(
    tokens, norm_gain, router_weight, gate_proj, up_proj, down_proj, expert_ids, slots, capacity
):
    tok_rows, shard_width = tokens.shape
    model_width = norm_gain.shape[0]
    experts = router_weight.shape[1]
    n_mp = model_width // shard_width
    slot_count = 4 * tok_rows // (3 * experts)
    cells = experts * slot_count
    me = lax.axis_index("expert")

    onehot = expert_ids[:, None] == jnp.arange(experts, dtype=jnp.int32)[None, :]
    cap_token = jnp.sum(jnp.where(onehot, capacity[None, :], 0), axis=1)
    kept_rows = slots < cap_token
    target = expert_ids * slot_count + slots
    route = (
        (target[:, None] == jnp.arange(cells, dtype=jnp.int32)[None, :]) & kept_rows[:, None]
    ).astype(jnp.bfloat16)

    masked = lax.dot_general(
        route, tokens, (((0,), (0,)), ((), ())), preferred_element_type=jnp.float32
    ).astype(jnp.bfloat16)
    received = lax.all_to_all(
        masked.reshape(experts, slot_count, shard_width),
        "expert",
        split_axis=0,
        concat_axis=0,
        tiled=True,
    ).reshape(cells, shard_width)
    n_z = lax.psum(1, "mz")
    n_x = n_mp // n_z
    at_x = lax.axis_index("mx")
    x_width = model_width // n_x

    def rows_relative(w):
        return jnp.roll(w, -at_x * x_width, axis=0)

    halves = []
    for rows in (received[: cells // 2], received[cells // 2 :]):
        copies = jnp.broadcast_to(rows[None], (n_z,) + rows.shape)
        part = lax.all_to_all(copies, "mz", split_axis=0, concat_axis=0, tiled=True)
        spread = jnp.broadcast_to(part[None], (n_x,) + part.shape)
        gathered = lax.all_to_all(spread, "mx", split_axis=0, concat_axis=0, tiled=True)
        halves.append(gathered.reshape(n_mp, cells // 2, shard_width))
    hidden_halves = {}
    gate_parts = []
    for lower, whole in zip((True, False), halves):
        rows_half = whole.shape[1]
        features = jnp.transpose(whole, (1, 0, 2)).reshape(rows_half, model_width)
        features = features.astype(jnp.float32)
        mean_square = jnp.sum(features * features, axis=1) / model_width
        scale = lax.rsqrt(mean_square + norm_eps)
        normed = (features * scale[:, None] * norm_gain).astype(jnp.bfloat16)

        logits = jnp.dot(normed, router_weight, preferred_element_type=jnp.float32)
        picked = jnp.sum(
            jnp.where(jnp.arange(experts, dtype=jnp.int32)[None, :] == me, logits, 0.0), axis=1
        )
        gate_parts.append(jax.nn.sigmoid(picked))

        pre_gate = jnp.dot(normed, gate_proj[0], preferred_element_type=jnp.float32)
        pre_up = jnp.dot(normed, up_proj[0], preferred_element_type=jnp.float32)
        hidden_halves[lower] = (jax.nn.gelu(pre_gate, approximate=True) * pre_up).astype(
            jnp.bfloat16
        )
    gate_prob = jnp.concatenate(gate_parts)

    def x_term(k, lower):
        columns = lax.dynamic_slice_in_dim(
            down_proj[0], ((at_x + k) % n_x) * x_width, x_width, axis=1
        )
        return jnp.dot(hidden_halves[lower], columns, preferred_element_type=jnp.float32).astype(
            jnp.bfloat16
        )

    across_x = [part.astype(jnp.bfloat16) for part in ring_reduce_scatter(x_term, "mx", n_x)]

    across_x = jnp.concatenate(across_x, axis=0).reshape(cells, n_z, shard_width)
    z_terms = lax.all_to_all(
        jnp.transpose(across_x, (1, 0, 2)), "mz", split_axis=0, concat_axis=0, tiled=True
    )
    summed = jnp.sum(z_terms.astype(jnp.float32), axis=0).astype(jnp.bfloat16)
    gated = (gate_prob[:, None] * summed.astype(jnp.float32)).astype(jnp.bfloat16)

    returned = lax.all_to_all(
        gated.reshape(experts, slot_count, shard_width),
        "expert",
        split_axis=0,
        concat_axis=0,
        tiled=True,
    ).reshape(cells, shard_width)
    update = jnp.dot(route, returned, preferred_element_type=jnp.float32)
    return update.astype(jnp.bfloat16)


def solution(mesh):
    n_expert, n_mp = mesh.devices.shape
    n_x = len({device.coords[0] for device in mesh.devices[0]})
    split = Mesh(mesh.devices.reshape(n_expert, n_x, n_mp // n_x), ("expert", "mx", "mz"))
    mp = ("mx", "mz")
    in_specs = (
        P("expert", mp),
        P(),
        P(),
        P("expert", None, mp),
        P("expert", None, mp),
        P("expert", mp, None),
        P("expert"),
        P("expert"),
        P(),
    )
    out_specs = P("expert", mp)
    return jax.shard_map(shards, mesh=split, in_specs=in_specs, out_specs=out_specs, check_vma=False)
```
